32 devices in a mesh: expert: 8 (over z, y), dp: 4 (over x, core).
Axes of the slice: x: 2, y: 2, z: 4, core: 2. Of those that a mesh axis runs over, the one named last changes fastest.
Arguments:
- tokens: bfloat16 [4096, 2048], P(('expert', 'dp')), may hold values from -6 to 6
- routes: int32 [4096, 1], P(('expert', 'dp')), may hold values from 0 to 7; in each aligned block of 128 rows (0 to 127, 128 to 255, ...) at most 24 rows name the same one
- route_weight: float32 [4096, 1], P(('expert', 'dp')), may hold values from 0.25 to 1
- w_in: bfloat16 [8, 2048, 768], P('expert'), may hold values from -0.125 to 0.125
- w_out: bfloat16 [8, 2048, 384], P('expert'), may hold values from -0.3125 to 0.3125
- out_grad: bfloat16 [4096, 2048], P(('expert', 'dp')), may hold values from -6 to 6
Outputs:
- mixed: bfloat16 [4096, 2048], P(('expert', 'dp'))
- token_grad: bfloat16 [4096, 2048], P(('expert', 'dp'))
- grad_in: bfloat16 [8, 2048, 768], P('expert', 'dp')
- grad_out: bfloat16 [8, 2048, 384], P('expert', 'dp')
The draws below stay inside these ranges and needn't reach their ends.
Inputs may be any that keep to these rules, and one draw needn't show every extreme that they name: `routes`: in the 128 rows of one device no expert is named more than 24 times, and in every draw some device names some expert exactly 24 times.
All inputs are finite; a program needn't handle non-finite values.
Results may differ from the reference program's by a relative error of at most 0.02.
Values may be sent and summed in bfloat16 or wider, within the bound.
No kernel may reach another device: no remote copies, remote signals or barrier semaphores. Data moves between devices by JAX's collectives and lax.ppermute only.
A program may use at most 64 MiB of HBM per device.

```python
import math
import jax
import jax.numpy as jnp
import numpy as np
from jax import lax

D = 2048
FW = 384
TOK_DEV = 128
EXPERTS = 8
TOKENS = 4096
CAP = 24
N_EXPERT = 8
N_DP = 4


def strengthened(drawn, key, source, target, blocks, factor):
    def block_of(dim):
        return (jnp.arange(drawn.shape[dim]) // (drawn.shape[dim] // blocks)).reshape((-1,) + (1,) * (drawn.ndim - 1 - dim))

    one_side = jax.random.permutation(key, blocks)[block_of(target)]
    second = (block_of(target) + blocks // 2) % blocks
    return jnp.where((block_of(source) == one_side) | (block_of(source) == second), factor * drawn, drawn)


def level_of(rng, dims, split, smallest, top_value):
    level, own = 1.0, jax.random.fold_in(rng, 6)
    for axis_at, parts in split:
        heights = jnp.exp(jax.random.uniform(jax.random.fold_in(own, axis_at), (parts,), jnp.float32, smallest / len(split), top_value / len(split)))
        level = level * jnp.repeat(heights, dims[axis_at] // parts).reshape([-1 if axis == axis_at else 1 for axis in range(len(dims))])
    return level


def assign_block(stream_key, own, number, rows, number_of, top, most, skew):
    order = jax.random.permutation(stream_key, number_of)
    packed, usual = shares(number_of, rows * top, most, skew, True), shares(number_of, rows * top, most, skew, False)
    places = jnp.arange(number_of)

    def named(sizes, rotation):
        used = int((sizes > 0).sum())
        fixed = max(1, used // 4)
        moved = fixed + (places - fixed + rotation * (used - fixed)) % max(1, number_of - fixed)
        return jnp.zeros((number_of,), jnp.int32).at[order[jnp.where(places < fixed, places, moved)]].set(jnp.asarray(sizes, jnp.int32))

    sizes = jnp.where(number % 4 == 0, named(packed, number // 4), named(usual, number - number // 4 - 1))
    mixed = jax.random.permutation(jax.random.fold_in(own, 3), number_of)
    donor, sink = mixed[0:number_of // 2 * 2:2], mixed[1:number_of // 2 * 2:2]
    margin = jnp.minimum(sizes[donor] - 1, most - sizes[sink]) // 2
    margin = jnp.where((donor == order[0]) | (sink == order[0]) | (sizes[sink] == 0), 0, jnp.maximum(margin, 0))
    moved = jax.random.randint(jax.random.fold_in(own, 4), (number_of // 2,), 0, 1 << 20) % (margin + 1)
    sizes = sizes.at[donor].add(-moved).at[sink].add(moved)
    labels = jnp.searchsorted(jnp.cumsum(sizes), jnp.arange(rows * top), side="right").astype(jnp.int32)
    grid = labels.reshape(top, rows).T
    grid = grid[jax.random.permutation(jax.random.fold_in(own, 1), rows)]
    rotation = jax.random.randint(jax.random.fold_in(own, 2), (rows, 1), 0, top)
    return jnp.take_along_axis(grid, (jnp.arange(top)[None, :] + rotation) % top, axis=1)


def shares(amount, total, reach, skew, full):
    loads = [(1 << 20) // math.isqrt(grade ** skew) + 1 for grade in range(1, amount + 1)]
    largest = reach if full else min(reach, max(-(-total // amount), total * loads[0] // sum(loads)))
    least = 1 if total - largest >= amount - 1 else 0
    counts, surplus = [largest] + [least] * (amount - 1), total - largest - least * (amount - 1)
    while surplus > 0:
        movable = [i for i in range(1, amount) if counts[i] < largest] or [i for i in range(1, amount) if counts[i] < reach]
        mass, left = sum([loads[i] for i in movable]), surplus
        for i in movable:
            more = min(reach - counts[i], max(1, left * loads[i] // mass), surplus)
            counts[i] = counts[i] + more
            surplus = surplus - more
    return np.array(counts)


def scatter_about(rng, shape, scale, bound, cuts=(), held_as=jnp.bfloat16):
    entries = jax.random.normal(rng, shape, jnp.float32) * scale
    if len(cuts) > 0:
        entries = level_of(rng, shape, cuts, -0.22, 0.18) * entries
    return jnp.clip(entries, min=-bound, max=bound).astype(held_as)


def noise_with(stream_key, extent, scale, limit, shards, heavy, kind=jnp.bfloat16):
    result = scale * jax.random.normal(stream_key, extent, jnp.float32)
    if shards:
        result = result * level_of(stream_key, extent, shards, -0.22, 0.18)
    return jnp.clip(strengthened(result, jax.random.fold_in(stream_key, 3), *heavy), -limit, limit).astype(kind)


def setup_inputs(seed: int = 0) -> dict:
    arg_keys = jax.random.split(jax.random.key(seed), 7)
    tokens = noise_with(arg_keys[0], (TOKENS, D), 1.0, 6.0, ((0, 32),), (0, 1, 32, 2.75))
    routes_keys = jax.random.split(jax.random.fold_in(arg_keys[1], 1), TOKENS // TOK_DEV)
    routes_turns = jax.random.permutation(jax.random.fold_in(arg_keys[1], 3), TOKENS // TOK_DEV)
    routes = jax.vmap(lambda own, number: assign_block(jax.random.fold_in(arg_keys[1], 2), own, number, TOK_DEV, EXPERTS, 1, CAP, 2))(routes_keys, routes_turns).reshape((TOKENS, 1))
    route_weight = jnp.clip(jnp.exp(math.log(1.0) - 1.3862944 * jax.random.uniform(arg_keys[2], (TOKENS, 1), jnp.float32) ** level_of(arg_keys[2], (TOKENS, 1), ((0, 32),), -0.2, 0.2)), 0.25, 1.0)
    w_in = scatter_about(arg_keys[3], (EXPERTS, D, 2 * FW), D ** -0.5, 0.125, ((0, 8),))
    w_out = scatter_about(arg_keys[4], (EXPERTS, D, FW), FW ** -0.5, 0.3125, ((0, 8),))
    out_grad = scatter_about(arg_keys[5], (TOKENS, D), 1.0, 6.0, ((0, 32),))
    return {"tokens": tokens, "routes": routes, "route_weight": route_weight, "w_in": w_in, "w_out": w_out, "out_grad": out_grad}


def rounded(value):
    return lax.optimization_barrier(value.astype(jnp.bfloat16)).astype(jnp.float32)


def placement_matrix(route_block, experts, capacity):
    chosen = route_block[:, 0]
    onehot = (chosen[:, None] == jnp.arange(experts, dtype=jnp.int32)[None, :]).astype(jnp.int32)
    ranks = jnp.sum(jnp.cumsum(onehot, axis=0) * onehot, axis=1) - 1
    target = chosen * capacity + ranks
    slots = jnp.arange(experts * capacity, dtype=jnp.int32)
    return (slots[:, None] == target[None, :]).astype(jnp.float32)


def expert_pass(rows_in, rows_cot, w_first, w_second):
    width = w_second.shape[2]
    gate_up = jnp.einsum("erd,edf->erf", rows_in, w_first)
    gate = gate_up[..., :width]
    upper = gate_up[..., width:]
    sigmoid_gate = jax.nn.sigmoid(gate)
    activated = gate * sigmoid_gate
    hidden = rounded(activated * upper)
    outputs = rounded(jnp.einsum("erf,edf->erd", hidden, w_second))
    grad_hidden = jnp.einsum("erd,edf->erf", rows_cot, w_second)
    grad_gate = grad_hidden * upper * sigmoid_gate * (1.0 + gate * (1.0 - sigmoid_gate))
    grad_upper = grad_hidden * activated
    grad_both = rounded(jnp.concatenate([grad_gate, grad_upper], axis=-1))
    grad_rows = rounded(jnp.einsum("erf,edf->erd", grad_both, w_first))
    term_first = jnp.einsum("erd,erf->edf", rows_in, grad_both)
    term_second = jnp.einsum("erd,erf->edf", rows_cot, hidden)
    return outputs, grad_rows, term_first, term_second


def reference(tokens, routes, route_weight, w_in, w_out, out_grad):
    token_parts = tokens.astype(jnp.float32).reshape(N_EXPERT, N_DP, TOK_DEV, D).transpose(1, 0, 2, 3)
    cotangent = rounded(route_weight * out_grad.astype(jnp.float32))
    cot_parts = cotangent.reshape(N_EXPERT, N_DP, TOK_DEV, D).transpose(1, 0, 2, 3)
    route_parts = routes.reshape(N_EXPERT, N_DP, TOK_DEV, 1).transpose(1, 0, 2, 3)
    w_first = w_in.astype(jnp.float32)
    w_second = w_out.astype(jnp.float32)

    def one_replica(carry, inputs):
        token_block, cot_block, route_block = inputs
        placer = jax.vmap(lambda block: placement_matrix(block, EXPERTS, CAP))(route_block)

        def to_experts(values):
            sent = jnp.einsum("jct,jtd->jcd", placer, values)
            sent = sent.reshape(N_EXPERT, EXPERTS, CAP, D).transpose(1, 0, 2, 3)
            return sent.reshape(EXPERTS, N_EXPERT * CAP, D)

        def to_tokens(values):
            back = values.reshape(EXPERTS, N_EXPERT, CAP, D).transpose(1, 0, 2, 3)
            back = back.reshape(N_EXPERT, EXPERTS * CAP, D)
            return jnp.einsum("jct,jcd->jtd", placer, back)

        outputs, grad_rows, term_first, term_second = expert_pass(
            to_experts(token_block), to_experts(cot_block), w_first, w_second)
        acc_first, acc_second = carry
        acc_first = acc_first + rounded(term_first)
        acc_second = acc_second + rounded(term_second)
        return (acc_first, acc_second), (to_tokens(outputs), to_tokens(grad_rows))

    start = (jnp.zeros((EXPERTS, D, 2 * FW), jnp.float32), jnp.zeros((EXPERTS, D, FW), jnp.float32))
    (acc_first, acc_second), (token_out, token_back) = lax.scan(one_replica, start, (token_parts, cot_parts, route_parts))
    token_out = token_out.transpose(1, 0, 2, 3).reshape(TOKENS, D)
    token_back = token_back.transpose(1, 0, 2, 3).reshape(TOKENS, D)
    mixed = (route_weight * token_out).astype(jnp.bfloat16)
    token_grad = token_back.astype(jnp.bfloat16)
    grad_in = (acc_first / N_DP).astype(jnp.bfloat16)
    grad_out = (acc_second / N_DP).astype(jnp.bfloat16)
    return (mixed, token_grad, grad_in, grad_out)
```

```python
import jax
import jax.numpy as jnp
from jax import lax
from jax.sharding import PartitionSpec as P


def placement_rows(routes, experts, capacity):
    chosen = routes[:, 0]
    onehot = (chosen[:, None] == jnp.arange(experts, dtype=jnp.int32)[None, :]).astype(jnp.int32)
    ranks = jnp.sum(jnp.cumsum(onehot, axis=0) * onehot, axis=1) - 1
    target = chosen * capacity + ranks
    slots = jnp.arange(experts * capacity, dtype=jnp.int32)
    return (slots[:, None] == target[None, :]).astype(jnp.bfloat16)


def contract_rows(left, right):
    return lax.dot_general(
        left, right, (((0,), (0,)), ((), ())), preferred_element_type=jnp.float32
    )


def contract_cols(left, right):
    return lax.dot_general(
        left, right, (((1,), (1,)), ((), ())), preferred_element_type=jnp.float32
    )


def reduce_scatter_rows(term, axis):
    size = lax.axis_size(axis)
    me = lax.axis_index(axis)
    bits = size.bit_length() - 1
    rows, cols = term.shape
    share = rows // size
    kept = term.reshape(size, share, cols)
    for b in range(bits):
        step = 1 << b
        halves = kept.reshape(kept.shape[0] // 2, 2, share, cols)
        mine = (me // step) % 2
        own = jnp.where(mine == 0, halves[:, 0], halves[:, 1])
        other = jnp.where(mine == 0, halves[:, 1], halves[:, 0])
        perm = [(k, k ^ step) for k in range(size)]
        got = lax.ppermute(other.astype(jnp.bfloat16), axis, perm)
        kept = own + got.astype(jnp.float32)
    return kept.reshape(share, cols)


def per_device(tokens, routes, route_weight, w_in, w_out, out_grad):
    token_count, model = tokens.shape
    experts = w_in.shape[0] * lax.axis_size("expert")
    capacity = 3 * token_count // (2 * experts)
    width = w_out.shape[2]
    replicas = lax.axis_size("dp")
    first = w_in[0]
    second = w_out[0]
    placer = placement_rows(routes, experts, capacity)
    cotangent = (route_weight * out_grad.astype(jnp.float32)).astype(jnp.bfloat16)
    both = jnp.concatenate([tokens, cotangent], axis=1)
    send = jnp.dot(placer, both, preferred_element_type=jnp.float32).astype(jnp.bfloat16)
    recv = lax.all_to_all(send, "expert", split_axis=0, concat_axis=0, tiled=True)
    rows_in = recv[:, :model]
    rows_cot = recv[:, model:]
    gate_up = jnp.dot(rows_in, first, preferred_element_type=jnp.float32)
    gate = gate_up[:, :width]
    upper = gate_up[:, width:]
    sigmoid_gate = jax.nn.sigmoid(gate)
    activated = gate * sigmoid_gate
    hidden = (activated * upper).astype(jnp.bfloat16)
    outputs = contract_cols(hidden, second).astype(jnp.bfloat16)
    grad_hidden = jnp.dot(rows_cot, second, preferred_element_type=jnp.float32)
    grad_gate = grad_hidden * upper * sigmoid_gate * (1.0 + gate * (1.0 - sigmoid_gate))
    grad_upper = grad_hidden * activated
    grad_both = jnp.concatenate([grad_gate, grad_upper], axis=1).astype(jnp.bfloat16)
    grad_rows = contract_cols(grad_both, first).astype(jnp.bfloat16)
    back = lax.all_to_all(
        jnp.concatenate([outputs, grad_rows], axis=1),
        "expert", split_axis=0, concat_axis=0, tiled=True,
    )
    token_back = contract_rows(placer, back)
    mixed = (route_weight * token_back[:, :model]).astype(jnp.bfloat16)
    token_grad = token_back[:, model:].astype(jnp.bfloat16)
    term_first = contract_rows(rows_in, grad_both).astype(jnp.bfloat16).astype(jnp.float32)
    term_second = contract_rows(rows_cot, hidden).astype(jnp.bfloat16).astype(jnp.float32)
    summed = reduce_scatter_rows(jnp.concatenate([term_first, term_second], axis=1), "dp")
    grad_in = (summed[:, : 2 * width] / replicas).astype(jnp.bfloat16)[None]
    grad_out = (summed[:, 2 * width :] / replicas).astype(jnp.bfloat16)[None]
    return (mixed, token_grad, grad_in, grad_out)


def solution(mesh):
    in_specs = (
        P(("expert", "dp"), None),
        P(("expert", "dp"), None),
        P(("expert", "dp"), None),
        P("expert", None, None),
        P("expert", None, None),
        P(("expert", "dp"), None),
    )
    out_specs = (
        P(("expert", "dp"), None),
        P(("expert", "dp"), None),
        P("expert", "dp", None),
        P("expert", "dp", None),
    )
    return jax.shard_map(
        per_device, mesh=mesh, in_specs=in_specs, out_specs=out_specs, check_vma=False
    )
```

```python
import jax
import jax.numpy as jnp
from jax import lax
from jax.sharding import PartitionSpec as P


def placement_rows(routes, experts, capacity):
    chosen = routes[:, 0]
    onehot = (chosen[:, None] == jnp.arange(experts, dtype=jnp.int32)[None, :]).astype(jnp.int32)
    ranks = jnp.sum(jnp.cumsum(onehot, axis=0) * onehot, axis=1) - 1
    target = chosen * capacity + ranks
    slots = jnp.arange(experts * capacity, dtype=jnp.int32)
    return (slots[:, None] == target[None, :]).astype(jnp.bfloat16)


def contract_rows(left, right):
    return lax.dot_general(
        left, right, (((0,), (0,)), ((), ())), preferred_element_type=jnp.float32
    )


def contract_cols(left, right):
    return lax.dot_general(
        left, right, (((1,), (1,)), ((), ())), preferred_element_type=jnp.float32
    )


def reduce_scatter_rows(terms, axis):
    size = lax.axis_size(axis)
    me = lax.axis_index(axis)
    share = terms[0].shape[0] // size
    blocks = [[t[m * share:(m + 1) * share] for m in range(size)] for t in terms]
    step = 1
    while step < size:
        low = (me // step) % 2 == 0
        keep, send = [], []
        for parts in blocks:
            mine, other = [], []
            for m in range(0, len(parts), 2):
                a, b = parts[m], parts[m + 1]
                mine.append(jnp.where(low, a, b))
                other.append(jnp.where(low, b, a))
            keep.append(mine)
            send.append(jnp.concatenate(other, axis=0).astype(jnp.bfloat16))
        payload = jnp.concatenate(send, axis=1)
        perm = [(k, k ^ step) for k in range(size)]
        got = lax.ppermute(payload, axis, perm).astype(jnp.float32)
        blocks, col = [], 0
        for mine, piece in zip(keep, send):
            width = piece.shape[1]
            blocks.append([
                mine[j] + got[j * share:(j + 1) * share, col:col + width]
                for j in range(len(mine))
            ])
            col += width
        step *= 2
    return [parts[0] for parts in blocks]


def per_device(tokens, routes, route_weight, w_in, w_out, out_grad):
    token_count = tokens.shape[0]
    experts = w_in.shape[0] * lax.axis_size("expert")
    capacity = 3 * token_count // (2 * experts)
    width = w_out.shape[2]
    replicas = lax.axis_size("dp")
    first = w_in[0]
    second = w_out[0]
    placer = placement_rows(routes, experts, capacity)
    cotangent = (route_weight * out_grad.astype(jnp.float32)).astype(jnp.bfloat16)
    send_rows = jnp.dot(placer, tokens, preferred_element_type=jnp.float32).astype(jnp.bfloat16)
    rows_in = lax.all_to_all(send_rows, "expert", split_axis=0, concat_axis=0, tiled=True)
    send_cot = jnp.dot(placer, cotangent, preferred_element_type=jnp.float32).astype(jnp.bfloat16)
    rows_cot = lax.all_to_all(send_cot, "expert", split_axis=0, concat_axis=0, tiled=True)
    gate_up = jnp.dot(rows_in, first, preferred_element_type=jnp.float32)
    gate = gate_up[:, :width]
    upper = gate_up[:, width:]
    sigmoid_gate = jax.nn.sigmoid(gate)
    activated = gate * sigmoid_gate
    hidden = (activated * upper).astype(jnp.bfloat16)
    outputs = contract_cols(hidden, second).astype(jnp.bfloat16)
    grad_hidden = jnp.dot(rows_cot, second, preferred_element_type=jnp.float32)
    grad_gate = grad_hidden * upper * sigmoid_gate * (1.0 + gate * (1.0 - sigmoid_gate))
    grad_upper = grad_hidden * activated
    grad_both = jnp.concatenate([grad_gate, grad_upper], axis=1).astype(jnp.bfloat16)
    grad_rows = contract_cols(grad_both, first).astype(jnp.bfloat16)
    back_out = lax.all_to_all(outputs, "expert", split_axis=0, concat_axis=0, tiled=True)
    back_grad = lax.all_to_all(grad_rows, "expert", split_axis=0, concat_axis=0, tiled=True)
    mixed = (route_weight * contract_rows(placer, back_out)).astype(jnp.bfloat16)
    token_grad = contract_rows(placer, back_grad).astype(jnp.bfloat16)
    term_first = contract_rows(rows_in, grad_both).astype(jnp.bfloat16).astype(jnp.float32)
    term_second = contract_rows(rows_cot, hidden).astype(jnp.bfloat16).astype(jnp.float32)
    sum_first, sum_second = reduce_scatter_rows([term_first, term_second], "dp")
    grad_in = (sum_first / replicas).astype(jnp.bfloat16)[None]
    grad_out = (sum_second / replicas).astype(jnp.bfloat16)[None]
    return (mixed, token_grad, grad_in, grad_out)


def solution(mesh):
    in_specs = (
        P(("expert", "dp"), None),
        P(("expert", "dp"), None),
        P(("expert", "dp"), None),
        P("expert", None, None),
        P("expert", None, None),
        P(("expert", "dp"), None),
    )
    out_specs = (
        P(("expert", "dp"), None),
        P(("expert", "dp"), None),
        P("expert", "dp", None),
        P("expert", "dp", None),
    )
    return jax.shard_map(
        per_device, mesh=mesh, in_specs=in_specs, out_specs=out_specs, check_vma=False
    )
```

```python
import jax
import jax.numpy as jnp
from jax import lax
from jax.sharding import PartitionSpec as P


def placement_rows(routes, experts, capacity):
    chosen = routes[:, 0]
    onehot = (chosen[:, None] == jnp.arange(experts, dtype=jnp.int32)[None, :]).astype(jnp.int32)
    ranks = jnp.sum(jnp.cumsum(onehot, axis=0) * onehot, axis=1) - 1
    target = chosen * capacity + ranks
    slots = jnp.arange(experts * capacity, dtype=jnp.int32)
    return (slots[:, None] == target[None, :]).astype(jnp.bfloat16)


def contract_rows(left, right):
    return lax.dot_general(
        left, right, (((0,), (0,)), ((), ())), preferred_element_type=jnp.float32
    )


def contract_cols(left, right):
    return lax.dot_general(
        left, right, (((1,), (1,)), ((), ())), preferred_element_type=jnp.float32
    )


def halving_order(rows, axis):
    size = lax.axis_size(axis)
    me = lax.axis_index(axis)
    bits = size.bit_length() - 1
    share = rows.shape[1] // size
    parts = []
    for p in range(size):
        rev = int(format(p, "0{}b".format(bits))[::-1], 2) if bits else 0
        start = (me ^ rev) * share
        parts.append(lax.dynamic_slice_in_dim(rows, start, share, axis=1))
    return jnp.concatenate(parts, axis=1)


def reduce_scatter_rows(terms, axis):
    size = lax.axis_size(axis)
    step = 1
    kept = terms
    while step < size:
        half = kept[0].shape[0] // 2
        perm = [(k, k ^ step) for k in range(size)]
        got = [lax.ppermute(t[half:].astype(jnp.bfloat16), axis, perm) for t in kept]
        kept = [t[:half].astype(jnp.float32) + g.astype(jnp.float32) for t, g in zip(kept, got)]
        step *= 2
    return kept


def per_device(tokens, routes, route_weight, w_in, w_out, out_grad):
    token_count = tokens.shape[0]
    experts = w_in.shape[0] * lax.axis_size("expert")
    capacity = 3 * token_count // (2 * experts)
    width = w_out.shape[2]
    replicas = lax.axis_size("dp")
    first = w_in[0]
    second = w_out[0]
    placer = placement_rows(routes, experts, capacity)
    cotangent = (route_weight * out_grad.astype(jnp.float32)).astype(jnp.bfloat16)
    send_rows = jnp.dot(placer, tokens, preferred_element_type=jnp.float32).astype(jnp.bfloat16)
    rows_in = lax.all_to_all(send_rows, "expert", split_axis=0, concat_axis=0, tiled=True)
    send_cot = jnp.dot(placer, cotangent, preferred_element_type=jnp.float32).astype(jnp.bfloat16)
    rows_cot = lax.all_to_all(send_cot, "expert", split_axis=0, concat_axis=0, tiled=True)
    gate_up = jnp.dot(rows_in, first, preferred_element_type=jnp.float32)
    gate = gate_up[:, :width]
    upper = gate_up[:, width:]
    sigmoid_gate = jax.nn.sigmoid(gate)
    activated = gate * sigmoid_gate
    hidden = (activated * upper).astype(jnp.bfloat16)
    outputs = contract_cols(hidden, second).astype(jnp.bfloat16)
    grad_hidden = jnp.dot(rows_cot, second, preferred_element_type=jnp.float32)
    grad_gate = grad_hidden * upper * sigmoid_gate * (1.0 + gate * (1.0 - sigmoid_gate))
    grad_upper = grad_hidden * activated
    grad_both = jnp.concatenate([grad_gate, grad_upper], axis=1).astype(jnp.bfloat16)
    grad_rows = contract_cols(grad_both, first).astype(jnp.bfloat16)
    back_out = lax.all_to_all(outputs, "expert", split_axis=0, concat_axis=0, tiled=True)
    back_grad = lax.all_to_all(grad_rows, "expert", split_axis=0, concat_axis=0, tiled=True)
    mixed = (route_weight * contract_rows(placer, back_out)).astype(jnp.bfloat16)
    token_grad = contract_rows(placer, back_grad).astype(jnp.bfloat16)
    term_first = contract_rows(halving_order(rows_in, "dp"), grad_both).astype(jnp.bfloat16)
    term_second = contract_rows(halving_order(rows_cot, "dp"), hidden).astype(jnp.bfloat16)
    sum_first, sum_second = reduce_scatter_rows([term_first, term_second], "dp")
    grad_in = (sum_first / replicas).astype(jnp.bfloat16)[None]
    grad_out = (sum_second / replicas).astype(jnp.bfloat16)[None]
    return (mixed, token_grad, grad_in, grad_out)


def solution(mesh):
    in_specs = (
        P(("expert", "dp"), None),
        P(("expert", "dp"), None),
        P(("expert", "dp"), None),
        P("expert", None, None),
        P("expert", None, None),
        P(("expert", "dp"), None),
    )
    out_specs = (
        P(("expert", "dp"), None),
        P(("expert", "dp"), None),
        P("expert", "dp", None),
        P("expert", "dp", None),
    )
    return jax.shard_map(
        per_device, mesh=mesh, in_specs=in_specs, out_specs=out_specs, check_vma=False
    )
```

```python
import jax
import jax.numpy as jnp
from jax import lax
from jax.sharding import PartitionSpec as P


def placement_rows(routes, experts, capacity):
    chosen = routes[:, 0]
    onehot = (chosen[:, None] == jnp.arange(experts, dtype=jnp.int32)[None, :]).astype(jnp.int32)
    ranks = jnp.sum(jnp.cumsum(onehot, axis=0) * onehot, axis=1) - 1
    target = chosen * capacity + ranks
    slots = jnp.arange(experts * capacity, dtype=jnp.int32)
    return (slots[:, None] == target[None, :]).astype(jnp.bfloat16)


def contract_rows(left, right):
    return lax.dot_general(
        left, right, (((0,), (0,)), ((), ())), preferred_element_type=jnp.float32
    )


def contract_cols(left, right):
    return lax.dot_general(
        left, right, (((1,), (1,)), ((), ())), preferred_element_type=jnp.float32
    )


def halving_order(rows, axis):
    size = lax.axis_size(axis)
    me = lax.axis_index(axis)
    bits = size.bit_length() - 1
    share = rows.shape[1] // size
    parts = []
    for p in range(size):
        rev = int(format(p, "0{}b".format(bits))[::-1], 2) if bits else 0
        start = (me ^ rev) * share
        parts.append(lax.dynamic_slice_in_dim(rows, start, share, axis=1))
    return jnp.concatenate(parts, axis=1)


def reduce_scatter_rows(terms, axis):
    size = lax.axis_size(axis)
    step = 1
    kept = terms
    while step < size:
        half = kept[0].shape[0] // 2
        perm = [(k, k ^ step) for k in range(size)]
        got = [lax.ppermute(t[half:].astype(jnp.bfloat16), axis, perm) for t in kept]
        kept = [t[:half].astype(jnp.float32) + g.astype(jnp.float32) for t, g in zip(kept, got)]
        step *= 2
    return kept


def per_device(tokens, routes, route_weight, w_in, w_out, out_grad):
    token_count, model = tokens.shape
    experts = w_in.shape[0] * lax.axis_size("expert")
    capacity = 3 * token_count // (2 * experts)
    width = w_out.shape[2]
    replicas = lax.axis_size("dp")
    first = w_in[0]
    second = w_out[0]
    placer = placement_rows(routes, experts, capacity)
    cotangent = (route_weight * out_grad.astype(jnp.float32)).astype(jnp.bfloat16)
    both = jnp.concatenate([tokens, cotangent], axis=1)
    send = jnp.dot(placer, both, preferred_element_type=jnp.float32).astype(jnp.bfloat16)
    recv = lax.all_to_all(send, "expert", split_axis=0, concat_axis=0, tiled=True)
    rows_in = recv[:, :model]
    rows_cot = recv[:, model:]
    gate_up = jnp.dot(rows_in, first, preferred_element_type=jnp.float32)
    gate = gate_up[:, :width]
    upper = gate_up[:, width:]
    sigmoid_gate = jax.nn.sigmoid(gate)
    activated = gate * sigmoid_gate
    hidden = (activated * upper).astype(jnp.bfloat16)
    outputs = contract_cols(hidden, second).astype(jnp.bfloat16)
    grad_hidden = jnp.dot(rows_cot, second, preferred_element_type=jnp.float32)
    grad_gate = grad_hidden * upper * sigmoid_gate * (1.0 + gate * (1.0 - sigmoid_gate))
    grad_upper = grad_hidden * activated
    grad_both = jnp.concatenate([grad_gate, grad_upper], axis=1).astype(jnp.bfloat16)
    grad_rows = contract_cols(grad_both, first).astype(jnp.bfloat16)
    back = lax.all_to_all(
        jnp.concatenate([outputs, grad_rows], axis=1),
        "expert", split_axis=0, concat_axis=0, tiled=True,
    )
    token_back = contract_rows(placer, back)
    mixed = (route_weight * token_back[:, :model]).astype(jnp.bfloat16)
    token_grad = token_back[:, model:].astype(jnp.bfloat16)
    term_first = contract_rows(halving_order(rows_in, "dp"), grad_both).astype(jnp.bfloat16)
    term_second = contract_rows(halving_order(rows_cot, "dp"), hidden).astype(jnp.bfloat16)
    sum_first, sum_second = reduce_scatter_rows([term_first, term_second], "dp")
    grad_in = (sum_first / replicas).astype(jnp.bfloat16)[None]
    grad_out = (sum_second / replicas).astype(jnp.bfloat16)[None]
    return (mixed, token_grad, grad_in, grad_out)


def solution(mesh):
    in_specs = (
        P(("expert", "dp"), None),
        P(("expert", "dp"), None),
        P(("expert", "dp"), None),
        P("expert", None, None),
        P("expert", None, None),
        P(("expert", "dp"), None),
    )
    out_specs = (
        P(("expert", "dp"), None),
        P(("expert", "dp"), None),
        P("expert", "dp", None),
        P("expert", "dp", None),
    )
    return jax.shard_map(
        per_device, mesh=mesh, in_specs=in_specs, out_specs=out_specs, check_vma=False
    )
```

```python
import jax
import jax.numpy as jnp
from jax import lax
from jax.sharding import PartitionSpec as P


def placement_chunks(routes, experts, capacity, chunks):
    chosen = routes[:, 0]
    onehot = (chosen[:, None] == jnp.arange(experts, dtype=jnp.int32)[None, :]).astype(jnp.int32)
    ranks = jnp.sum(jnp.cumsum(onehot, axis=0) * onehot, axis=1) - 1
    target = chosen * capacity + ranks
    per = capacity // chunks
    placers = []
    for c in range(chunks):
        slots = (jnp.arange(experts, dtype=jnp.int32)[:, None] * capacity
                 + c * per + jnp.arange(per, dtype=jnp.int32)[None, :]).reshape(-1)
        placers.append((slots[:, None] == target[None, :]).astype(jnp.bfloat16))
    return placers


def contract_rows(left, right):
    return lax.dot_general(
        left, right, (((0,), (0,)), ((), ())), preferred_element_type=jnp.float32
    )


def contract_cols(left, right):
    return lax.dot_general(
        left, right, (((1,), (1,)), ((), ())), preferred_element_type=jnp.float32
    )


def halving_order(rows, axis):
    size = lax.axis_size(axis)
    me = lax.axis_index(axis)
    bits = size.bit_length() - 1
    share = rows.shape[1] // size
    parts = []
    for p in range(size):
        rev = int(format(p, "0{}b".format(bits))[::-1], 2) if bits else 0
        start = (me ^ rev) * share
        parts.append(lax.dynamic_slice_in_dim(rows, start, share, axis=1))
    return jnp.concatenate(parts, axis=1)


def reduce_scatter_rows(terms, axis):
    size = lax.axis_size(axis)
    step = 1
    kept = terms
    while step < size:
        half = kept[0].shape[0] // 2
        perm = [(k, k ^ step) for k in range(size)]
        got = [lax.ppermute(t[half:].astype(jnp.bfloat16), axis, perm) for t in kept]
        kept = [t[:half].astype(jnp.float32) + g.astype(jnp.float32) for t, g in zip(kept, got)]
        step *= 2
    return kept


def expert_rows(recv, first, second, model, width):
    rows_in = recv[:, :model]
    rows_cot = recv[:, model:]
    gate_up = jnp.dot(rows_in, first, preferred_element_type=jnp.float32)
    gate = gate_up[:, :width]
    upper = gate_up[:, width:]
    sigmoid_gate = jax.nn.sigmoid(gate)
    activated = gate * sigmoid_gate
    hidden = (activated * upper).astype(jnp.bfloat16)
    outputs = contract_cols(hidden, second).astype(jnp.bfloat16)
    grad_hidden = jnp.dot(rows_cot, second, preferred_element_type=jnp.float32)
    grad_gate = grad_hidden * upper * sigmoid_gate * (1.0 + gate * (1.0 - sigmoid_gate))
    grad_upper = grad_hidden * activated
    grad_both = jnp.concatenate([grad_gate, grad_upper], axis=1).astype(jnp.bfloat16)
    grad_rows = contract_cols(grad_both, first).astype(jnp.bfloat16)
    return rows_in, rows_cot, hidden, grad_both, jnp.concatenate([outputs, grad_rows], axis=1)


def per_device(tokens, routes, route_weight, w_in, w_out, out_grad):
    token_count, model = tokens.shape
    experts = w_in.shape[0] * lax.axis_size("expert")
    capacity = 3 * token_count // (2 * experts)
    width = w_out.shape[2]
    replicas = lax.axis_size("dp")
    first = w_in[0]
    second = w_out[0]
    placers = placement_chunks(routes, experts, capacity, 2)
    cotangent = (route_weight * out_grad.astype(jnp.float32)).astype(jnp.bfloat16)
    both = jnp.concatenate([tokens, cotangent], axis=1)
    received = [
        lax.all_to_all(
            jnp.dot(placer, both, preferred_element_type=jnp.float32).astype(jnp.bfloat16),
            "expert", split_axis=0, concat_axis=0, tiled=True,
        )
        for placer in placers
    ]
    pieces, backs = [], []
    token_back = None
    for c, placer in enumerate(placers):
        rows_in, rows_cot, hidden, grad_both, result = expert_rows(received[c], first, second, model, width)
        if c + 1 < len(placers):
            result, received[c + 1] = lax.optimization_barrier((result, received[c + 1]))
        pieces.append((rows_in, rows_cot, hidden, grad_both))
        if backs:
            result, backs[-1] = lax.optimization_barrier((result, backs[-1]))
        backs.append(lax.all_to_all(result, "expert", split_axis=0, concat_axis=0, tiled=True))
    for placer, back in zip(placers, backs):
        part = contract_rows(placer, back)
        token_back = part if token_back is None else token_back + part
    mixed = (route_weight * token_back[:, :model]).astype(jnp.bfloat16)
    token_grad = token_back[:, model:].astype(jnp.bfloat16)
    rows_in, rows_cot, hidden, grad_both = [jnp.concatenate(x, axis=0) for x in zip(*pieces)]
    term_first = contract_rows(halving_order(rows_in, "dp"), grad_both).astype(jnp.bfloat16)
    term_second = contract_rows(halving_order(rows_cot, "dp"), hidden).astype(jnp.bfloat16)
    sum_first, sum_second = reduce_scatter_rows([term_first, term_second], "dp")
    grad_in = (sum_first / replicas).astype(jnp.bfloat16)[None]
    grad_out = (sum_second / replicas).astype(jnp.bfloat16)[None]
    return (mixed, token_grad, grad_in, grad_out)


def solution(mesh):
    in_specs = (
        P(("expert", "dp"), None),
        P(("expert", "dp"), None),
        P(("expert", "dp"), None),
        P("expert", None, None),
        P("expert", None, None),
        P(("expert", "dp"), None),
    )
    out_specs = (
        P(("expert", "dp"), None),
        P(("expert", "dp"), None),
        P("expert", "dp", None),
        P("expert", "dp", None),
    )
    return jax.shard_map(
        per_device, mesh=mesh, in_specs=in_specs, out_specs=out_specs, check_vma=False
    )
```

```python
import jax
import jax.numpy as jnp
from jax import lax
from jax.sharding import PartitionSpec as P


def placement_rows(routes, experts, capacity):
    chosen = routes[:, 0]
    onehot = (chosen[:, None] == jnp.arange(experts, dtype=jnp.int32)[None, :]).astype(jnp.int32)
    ranks = jnp.sum(jnp.cumsum(onehot, axis=0) * onehot, axis=1) - 1
    target = chosen * capacity + ranks
    slots = jnp.arange(experts * capacity, dtype=jnp.int32)
    return (slots[:, None] == target[None, :]).astype(jnp.bfloat16)


def contract_rows(left, right):
    return lax.dot_general(
        left, right, (((0,), (0,)), ((), ())), preferred_element_type=jnp.float32
    )


def contract_cols(left, right):
    return lax.dot_general(
        left, right, (((1,), (1,)), ((), ())), preferred_element_type=jnp.float32
    )


def halving_order(rows, axis):
    size = lax.axis_size(axis)
    me = lax.axis_index(axis)
    bits = size.bit_length() - 1
    share = rows.shape[1] // size
    parts = []
    for p in range(size):
        rev = int(format(p, "0{}b".format(bits))[::-1], 2) if bits else 0
        start = (me ^ rev) * share
        parts.append(lax.dynamic_slice_in_dim(rows, start, share, axis=1))
    return jnp.concatenate(parts, axis=1)


def reduce_scatter_rows(terms, axis):
    size = lax.axis_size(axis)
    step = 1
    kept = terms
    while step < size:
        half = kept[0].shape[0] // 2
        perm = [(k, k ^ step) for k in range(size)]
        got = [lax.ppermute(t[half:].astype(jnp.bfloat16), axis, perm) for t in kept]
        kept = [t[:half].astype(jnp.float32) + g.astype(jnp.float32) for t, g in zip(kept, got)]
        step *= 2
    return kept


def per_device(tokens, routes, route_weight, w_in, w_out, out_grad):
    token_count, model = tokens.shape
    experts = w_in.shape[0] * lax.axis_size("expert")
    capacity = 3 * token_count // (2 * experts)
    width = w_out.shape[2]
    replicas = lax.axis_size("dp")
    first = w_in[0]
    second = w_out[0]
    placer = placement_rows(routes, experts, capacity)
    cotangent = (route_weight * out_grad.astype(jnp.float32)).astype(jnp.bfloat16)
    both = jnp.concatenate([tokens, cotangent], axis=1)
    send = jnp.dot(placer, both, preferred_element_type=jnp.float32).astype(jnp.bfloat16)
    recv = lax.all_to_all(send, "expert", split_axis=0, concat_axis=0, tiled=True)
    rows_in = recv[:, :model]
    rows_cot = recv[:, model:]
    gate_up = jnp.dot(rows_in, first, preferred_element_type=jnp.float32)
    gate = gate_up[:, :width]
    upper = gate_up[:, width:]
    sigmoid_gate = jax.nn.sigmoid(gate)
    activated = gate * sigmoid_gate
    hidden = (activated * upper).astype(jnp.bfloat16)
    outputs = contract_cols(hidden, second).astype(jnp.bfloat16)
    grad_hidden = jnp.dot(rows_cot, second, preferred_element_type=jnp.float32)
    grad_gate = grad_hidden * upper * sigmoid_gate * (1.0 + gate * (1.0 - sigmoid_gate))
    grad_upper = grad_hidden * activated
    grad_both = jnp.concatenate([grad_gate, grad_upper], axis=1).astype(jnp.bfloat16)
    grad_rows = contract_cols(grad_both, first).astype(jnp.bfloat16)
    back_out = lax.all_to_all(outputs, "expert", split_axis=0, concat_axis=0, tiled=True)
    grad_rows, back_out = lax.optimization_barrier((grad_rows, back_out))
    back_grad = lax.all_to_all(grad_rows, "expert", split_axis=0, concat_axis=0, tiled=True)
    mixed = (route_weight * contract_rows(placer, back_out)).astype(jnp.bfloat16)
    token_grad = contract_rows(placer, back_grad).astype(jnp.bfloat16)
    term_first = contract_rows(halving_order(rows_in, "dp"), grad_both).astype(jnp.bfloat16)
    term_second = contract_rows(halving_order(rows_cot, "dp"), hidden).astype(jnp.bfloat16)
    sum_first, sum_second = reduce_scatter_rows([term_first, term_second], "dp")
    grad_in = (sum_first / replicas).astype(jnp.bfloat16)[None]
    grad_out = (sum_second / replicas).astype(jnp.bfloat16)[None]
    return (mixed, token_grad, grad_in, grad_out)


def solution(mesh):
    in_specs = (
        P(("expert", "dp"), None),
        P(("expert", "dp"), None),
        P(("expert", "dp"), None),
        P("expert", None, None),
        P("expert", None, None),
        P(("expert", "dp"), None),
    )
    out_specs = (
        P(("expert", "dp"), None),
        P(("expert", "dp"), None),
        P("expert", "dp", None),
        P("expert", "dp", None),
    )
    return jax.shard_map(
        per_device, mesh=mesh, in_specs=in_specs, out_specs=out_specs, check_vma=False
    )
```

```python
import jax
import jax.numpy as jnp
from jax import lax
from jax.sharding import PartitionSpec as P


def placement_rows(routes, experts, capacity):
    chosen = routes[:, 0]
    onehot = (chosen[:, None] == jnp.arange(experts, dtype=jnp.int32)[None, :]).astype(jnp.int32)
    ranks = jnp.sum(jnp.cumsum(onehot, axis=0) * onehot, axis=1) - 1
    target = chosen * capacity + ranks
    slots = jnp.arange(experts * capacity, dtype=jnp.int32)
    return (slots[:, None] == target[None, :]).astype(jnp.bfloat16)


def contract_rows(left, right):
    return lax.dot_general(
        left, right, (((0,), (0,)), ((), ())), preferred_element_type=jnp.float32
    )


def contract_cols(left, right):
    return lax.dot_general(
        left, right, (((1,), (1,)), ((), ())), preferred_element_type=jnp.float32
    )


def halving_order(rows, axis):
    size = lax.axis_size(axis)
    me = lax.axis_index(axis)
    bits = size.bit_length() - 1
    share = rows.shape[1] // size
    parts = []
    for p in range(size):
        rev = int(format(p, "0{}b".format(bits))[::-1], 2) if bits else 0
        start = (me ^ rev) * share
        parts.append(lax.dynamic_slice_in_dim(rows, start, share, axis=1))
    return jnp.concatenate(parts, axis=1)


def reduce_scatter_rows(terms, axis):
    size = lax.axis_size(axis)
    step = 1
    kept = terms
    while step < size:
        half = kept[0].shape[0] // 2
        perm = [(k, k ^ step) for k in range(size)]
        got = [lax.ppermute(t[half:].astype(jnp.bfloat16), axis, perm) for t in kept]
        kept = [t[:half].astype(jnp.float32) + g.astype(jnp.float32) for t, g in zip(kept, got)]
        step *= 2
    return kept


def per_device(tokens, routes, route_weight, w_in, w_out, out_grad):
    token_count, model = tokens.shape
    experts = w_in.shape[0] * lax.axis_size("expert")
    capacity = 3 * token_count // (2 * experts)
    width = w_out.shape[2]
    replicas = lax.axis_size("dp")
    first = w_in[0]
    second = w_out[0]
    placer = placement_rows(routes, experts, capacity)
    cotangent = (route_weight * out_grad.astype(jnp.float32)).astype(jnp.bfloat16)
    both = jnp.concatenate([tokens, cotangent], axis=1)
    send = jnp.dot(placer, both, preferred_element_type=jnp.float32).astype(jnp.bfloat16)
    recv = lax.all_to_all(send, "expert", split_axis=0, concat_axis=0, tiled=True)
    rows_in = recv[:, :model]
    rows_cot = recv[:, model:]
    gate_up = jnp.dot(rows_in, first, preferred_element_type=jnp.float32)
    gate = gate_up[:, :width]
    upper = gate_up[:, width:]
    sigmoid_gate = jax.nn.sigmoid(gate)
    activated = gate * sigmoid_gate
    hidden = (activated * upper).astype(jnp.bfloat16)
    outputs = contract_cols(hidden, second).astype(jnp.bfloat16)
    grad_hidden = jnp.dot(rows_cot, second, preferred_element_type=jnp.float32)
    grad_gate = grad_hidden * upper * sigmoid_gate * (1.0 + gate * (1.0 - sigmoid_gate))
    grad_upper = grad_hidden * activated
    grad_both = jnp.concatenate([grad_gate, grad_upper], axis=1).astype(jnp.bfloat16)
    grad_rows = contract_cols(grad_both, first).astype(jnp.bfloat16)
    payload = jnp.concatenate([outputs, grad_rows], axis=1)
    payload, rows_in, rows_cot, grad_both, hidden = lax.optimization_barrier(
        (payload, rows_in, rows_cot, grad_both, hidden))
    back = lax.all_to_all(payload, "expert", split_axis=0, concat_axis=0, tiled=True)
    mixed = (route_weight * contract_rows(placer, back[:, :model])).astype(jnp.bfloat16)
    token_grad = contract_rows(placer, back[:, model:]).astype(jnp.bfloat16)
    term_first = contract_rows(halving_order(rows_in, "dp"), grad_both).astype(jnp.bfloat16)
    term_second = contract_rows(halving_order(rows_cot, "dp"), hidden).astype(jnp.bfloat16)
    sum_first, sum_second = reduce_scatter_rows([term_first, term_second], "dp")
    grad_in = (sum_first / replicas).astype(jnp.bfloat16)[None]
    grad_out = (sum_second / replicas).astype(jnp.bfloat16)[None]
    return (mixed, token_grad, grad_in, grad_out)


def solution(mesh):
    in_specs = (
        P(("expert", "dp"), None),
        P(("expert", "dp"), None),
        P(("expert", "dp"), None),
        P("expert", None, None),
        P("expert", None, None),
        P(("expert", "dp"), None),
    )
    out_specs = (
        P(("expert", "dp"), None),
        P(("expert", "dp"), None),
        P("expert", "dp", None),
        P("expert", "dp", None),
    )
    return jax.shard_map(
        per_device, mesh=mesh, in_specs=in_specs, out_specs=out_specs, check_vma=False
    )
```

```python
import jax
import jax.numpy as jnp
from jax import lax
from jax.experimental import pallas as pl
from jax.experimental.pallas import tpu as pltpu
from jax.sharding import PartitionSpec as P


def placement_rows(routes, experts, capacity):
    chosen = routes[:, 0]
    onehot = (chosen[:, None] == jnp.arange(experts, dtype=jnp.int32)[None, :]).astype(jnp.int32)
    ranks = jnp.sum(jnp.cumsum(onehot, axis=0) * onehot, axis=1) - 1
    target = chosen * capacity + ranks
    slots = jnp.arange(experts * capacity, dtype=jnp.int32)
    return (slots[:, None] == target[None, :]).astype(jnp.bfloat16)


def contract_rows(left, right):
    return lax.dot_general(
        left, right, (((0,), (0,)), ((), ())), preferred_element_type=jnp.float32
    )


def contract_cols(left, right):
    return lax.dot_general(
        left, right, (((1,), (1,)), ((), ())), preferred_element_type=jnp.float32
    )


def halving_order(rows, axis):
    size = lax.axis_size(axis)
    me = lax.axis_index(axis)
    bits = size.bit_length() - 1
    share = rows.shape[1] // size
    parts = []
    for p in range(size):
        rev = int(format(p, "0{}b".format(bits))[::-1], 2) if bits else 0
        start = (me ^ rev) * share
        parts.append(lax.dynamic_slice_in_dim(rows, start, share, axis=1))
    return jnp.concatenate(parts, axis=1)


def reduce_scatter_rows(terms, axis):
    size = lax.axis_size(axis)
    step = 1
    kept = terms
    while step < size:
        half = kept[0].shape[0] // 2
        perm = [(k, k ^ step) for k in range(size)]
        got = [lax.ppermute(t[half:].astype(jnp.bfloat16), axis, perm) for t in kept]
        kept = [t[:half].astype(jnp.float32) + g.astype(jnp.float32) for t, g in zip(kept, got)]
        step *= 2
    return kept


def expert_kernel(recv_ref, w_in_ref, w_out_ref, pay_ref, hid_ref, q_ref):
    model = w_in_ref.shape[0]
    width = w_out_ref.shape[1]
    w_in = w_in_ref[...]
    w_out = w_out_ref[...]
    gate_up = jnp.dot(recv_ref[:, :model], w_in, preferred_element_type=jnp.float32)
    gate = gate_up[:, :width]
    upper = gate_up[:, width:]
    sigmoid_gate = 1.0 / (1.0 + jnp.exp(-gate))
    activated = gate * sigmoid_gate
    hidden = (activated * upper).astype(jnp.bfloat16)
    hid_ref[...] = hidden
    pay_ref[:, :model] = contract_cols(hidden, w_out).astype(jnp.bfloat16)
    grad_hidden = jnp.dot(recv_ref[:, model:], w_out, preferred_element_type=jnp.float32)
    grad_gate = grad_hidden * upper * sigmoid_gate * (1.0 + gate * (1.0 - sigmoid_gate))
    q_ref[:, :width] = grad_gate.astype(jnp.bfloat16)
    q_ref[:, width:] = (grad_hidden * activated).astype(jnp.bfloat16)
    pay_ref[:, model:] = contract_cols(q_ref[...], w_in).astype(jnp.bfloat16)


def expert_rows(recv, first, second):
    rows = recv.shape[0]
    model, width = second.shape
    vmem = pl.BlockSpec(memory_space=pltpu.VMEM)
    flops = 2 * rows * model * width * 6
    moved = 2 * (2 * rows * 2 * model + model * 3 * width + rows * 3 * width)
    return pl.pallas_call(
        expert_kernel,
        out_shape=(
            jax.ShapeDtypeStruct((rows, 2 * model), jnp.bfloat16),
            jax.ShapeDtypeStruct((rows, width), jnp.bfloat16),
            jax.ShapeDtypeStruct((rows, 2 * width), jnp.bfloat16),
        ),
        in_specs=[vmem, vmem, vmem],
        out_specs=(vmem, vmem, vmem),
        cost_estimate=pl.CostEstimate(
            flops=flops, bytes_accessed=moved, transcendentals=rows * width),
    )(recv, first, second)


def per_device(tokens, routes, route_weight, w_in, w_out, out_grad):
    token_count, model = tokens.shape
    experts = w_in.shape[0] * lax.axis_size("expert")
    capacity = 3 * token_count // (2 * experts)
    width = w_out.shape[2]
    replicas = lax.axis_size("dp")
    first = w_in[0]
    second = w_out[0]
    placer = placement_rows(routes, experts, capacity)
    cotangent = (route_weight * out_grad.astype(jnp.float32)).astype(jnp.bfloat16)
    both = jnp.concatenate([tokens, cotangent], axis=1)
    send = jnp.dot(placer, both, preferred_element_type=jnp.float32).astype(jnp.bfloat16)
    recv = lax.all_to_all(send, "expert", split_axis=0, concat_axis=0, tiled=True)
    payload, hidden, grad_both = expert_rows(recv, first, second)
    rows_in = recv[:, :model]
    rows_cot = recv[:, model:]
    back = lax.all_to_all(payload, "expert", split_axis=0, concat_axis=0, tiled=True)
    token_back = contract_rows(placer, back)
    mixed = (route_weight * token_back[:, :model]).astype(jnp.bfloat16)
    token_grad = token_back[:, model:].astype(jnp.bfloat16)
    term_first = contract_rows(halving_order(rows_in, "dp"), grad_both).astype(jnp.bfloat16)
    term_second = contract_rows(halving_order(rows_cot, "dp"), hidden).astype(jnp.bfloat16)
    sum_first, sum_second = reduce_scatter_rows([term_first, term_second], "dp")
    grad_in = (sum_first / replicas).astype(jnp.bfloat16)[None]
    grad_out = (sum_second / replicas).astype(jnp.bfloat16)[None]
    return (mixed, token_grad, grad_in, grad_out)


def solution(mesh):
    in_specs = (
        P(("expert", "dp"), None),
        P(("expert", "dp"), None),
        P(("expert", "dp"), None),
        P("expert", None, None),
        P("expert", None, None),
        P(("expert", "dp"), None),
    )
    out_specs = (
        P(("expert", "dp"), None),
        P(("expert", "dp"), None),
        P("expert", "dp", None),
        P("expert", "dp", None),
    )
    return jax.shard_map(
        per_device, mesh=mesh, in_specs=in_specs, out_specs=out_specs, check_vma=False
    )
```

```python
import jax
import jax.numpy as jnp
from jax import lax
from jax.experimental import pallas as pl
from jax.experimental.pallas import tpu as pltpu
from jax.sharding import PartitionSpec as P


def placement_rows(routes, experts, capacity):
    chosen = routes[:, 0]
    onehot = (chosen[:, None] == jnp.arange(experts, dtype=jnp.int32)[None, :]).astype(jnp.float32)
    count = chosen.shape[0]
    earlier = (jnp.arange(count)[None, :] < jnp.arange(count)[:, None]).astype(jnp.float32)
    before = jnp.dot(earlier, onehot, precision=lax.Precision.HIGHEST)
    ranks = jnp.sum(before * onehot, axis=1).astype(jnp.int32)
    target = chosen * capacity + ranks
    slots = jnp.arange(experts * capacity, dtype=jnp.int32)
    return (slots[:, None] == target[None, :]).astype(jnp.bfloat16)


def contract_rows(left, right):
    return lax.dot_general(
        left, right, (((0,), (0,)), ((), ())), preferred_element_type=jnp.float32
    )


def contract_cols(left, right):
    return lax.dot_general(
        left, right, (((1,), (1,)), ((), ())), preferred_element_type=jnp.float32
    )


def halving_order(rows, axis):
    size = lax.axis_size(axis)
    me = lax.axis_index(axis)
    bits = size.bit_length() - 1
    share = rows.shape[1] // size
    parts = []
    for p in range(size):
        rev = int(format(p, "0{}b".format(bits))[::-1], 2) if bits else 0
        start = (me ^ rev) * share
        parts.append(lax.dynamic_slice_in_dim(rows, start, share, axis=1))
    return jnp.concatenate(parts, axis=1)


def reduce_scatter_rows(terms, axis):
    size = lax.axis_size(axis)
    step = 1
    kept = terms
    while step < size:
        half = kept[0].shape[0] // 2
        perm = [(k, k ^ step) for k in range(size)]
        got = [lax.ppermute(t[half:].astype(jnp.bfloat16), axis, perm) for t in kept]
        kept = [t[:half].astype(jnp.float32) + g.astype(jnp.float32) for t, g in zip(kept, got)]
        step *= 2
    return kept


def expert_kernel(recv_ref, w_in_ref, w_out_ref, pay_ref, hid_ref, q_ref):
    model = w_in_ref.shape[0]
    width = w_out_ref.shape[1]
    w_in = w_in_ref[...]
    w_out = w_out_ref[...]
    gate_up = jnp.dot(recv_ref[:, :model], w_in, preferred_element_type=jnp.float32)
    gate = gate_up[:, :width]
    upper = gate_up[:, width:]
    sigmoid_gate = 1.0 / (1.0 + jnp.exp(-gate))
    activated = gate * sigmoid_gate
    hidden = (activated * upper).astype(jnp.bfloat16)
    hid_ref[...] = hidden
    pay_ref[:, :model] = contract_cols(hidden, w_out).astype(jnp.bfloat16)
    grad_hidden = jnp.dot(recv_ref[:, model:], w_out, preferred_element_type=jnp.float32)
    grad_gate = grad_hidden * upper * sigmoid_gate * (1.0 + gate * (1.0 - sigmoid_gate))
    q_ref[:, :width] = grad_gate.astype(jnp.bfloat16)
    q_ref[:, width:] = (grad_hidden * activated).astype(jnp.bfloat16)
    pay_ref[:, model:] = contract_cols(q_ref[...], w_in).astype(jnp.bfloat16)


def expert_rows(recv, first, second):
    rows = recv.shape[0]
    model, width = second.shape
    vmem = pl.BlockSpec(memory_space=pltpu.VMEM)
    flops = 2 * rows * model * width * 6
    moved = 2 * (2 * rows * 2 * model + model * 3 * width + rows * 3 * width)
    return pl.pallas_call(
        expert_kernel,
        out_shape=(
            jax.ShapeDtypeStruct((rows, 2 * model), jnp.bfloat16),
            jax.ShapeDtypeStruct((rows, width), jnp.bfloat16),
            jax.ShapeDtypeStruct((rows, 2 * width), jnp.bfloat16),
        ),
        in_specs=[vmem, vmem, vmem],
        out_specs=(vmem, vmem, vmem),
        cost_estimate=pl.CostEstimate(
            flops=flops, bytes_accessed=moved, transcendentals=rows * width),
    )(recv, first, second)


def per_device(tokens, routes, route_weight, w_in, w_out, out_grad):
    token_count, model = tokens.shape
    experts = w_in.shape[0] * lax.axis_size("expert")
    capacity = 3 * token_count // (2 * experts)
    width = w_out.shape[2]
    replicas = lax.axis_size("dp")
    first = w_in[0]
    second = w_out[0]
    placer = placement_rows(routes, experts, capacity)
    cotangent = (route_weight * out_grad.astype(jnp.float32)).astype(jnp.bfloat16)
    both = jnp.concatenate([tokens, cotangent], axis=1)
    send = jnp.dot(placer, both, preferred_element_type=jnp.float32).astype(jnp.bfloat16)
    recv = lax.all_to_all(send, "expert", split_axis=0, concat_axis=0, tiled=True)
    payload, hidden, grad_both = expert_rows(recv, first, second)
    rows_in = recv[:, :model]
    rows_cot = recv[:, model:]
    back = lax.all_to_all(payload, "expert", split_axis=0, concat_axis=0, tiled=True)
    token_back = contract_rows(placer, back)
    mixed = (route_weight * token_back[:, :model]).astype(jnp.bfloat16)
    token_grad = token_back[:, model:].astype(jnp.bfloat16)
    term_first = contract_rows(halving_order(rows_in, "dp"), grad_both).astype(jnp.bfloat16)
    term_second = contract_rows(halving_order(rows_cot, "dp"), hidden).astype(jnp.bfloat16)
    sum_first, sum_second = reduce_scatter_rows([term_first, term_second], "dp")
    grad_in = (sum_first / replicas).astype(jnp.bfloat16)[None]
    grad_out = (sum_second / replicas).astype(jnp.bfloat16)[None]
    return (mixed, token_grad, grad_in, grad_out)


def solution(mesh):
    in_specs = (
        P(("expert", "dp"), None),
        P(("expert", "dp"), None),
        P(("expert", "dp"), None),
        P("expert", None, None),
        P("expert", None, None),
        P(("expert", "dp"), None),
    )
    out_specs = (
        P(("expert", "dp"), None),
        P(("expert", "dp"), None),
        P("expert", "dp", None),
        P("expert", "dp", None),
    )
    return jax.shard_map(
        per_device, mesh=mesh, in_specs=in_specs, out_specs=out_specs, check_vma=False
    )
```

```python
import jax
import jax.numpy as jnp
from jax import lax
from jax.experimental import pallas as pl
from jax.experimental.pallas import tpu as pltpu
from jax.sharding import PartitionSpec as P


def placement_rows(routes, experts, capacity):
    chosen = routes[:, 0]
    onehot = (chosen[:, None] == jnp.arange(experts, dtype=jnp.int32)[None, :]).astype(jnp.int32)
    ranks = jnp.sum(jnp.cumsum(onehot, axis=0) * onehot, axis=1) - 1
    target = chosen * capacity + ranks
    slots = jnp.arange(experts * capacity, dtype=jnp.int32)
    return (slots[:, None] == target[None, :]).astype(jnp.bfloat16)


def contract_rows(left, right):
    return lax.dot_general(
        left, right, (((0,), (0,)), ((), ())), preferred_element_type=jnp.float32
    )


def contract_cols(left, right):
    return lax.dot_general(
        left, right, (((1,), (1,)), ((), ())), preferred_element_type=jnp.float32
    )


def halving_order(rows, axis):
    size = lax.axis_size(axis)
    me = lax.axis_index(axis)
    bits = size.bit_length() - 1
    share = rows.shape[1] // size
    parts = []
    for p in range(size):
        rev = int(format(p, "0{}b".format(bits))[::-1], 2) if bits else 0
        start = (me ^ rev) * share
        parts.append(lax.dynamic_slice_in_dim(rows, start, share, axis=1))
    return jnp.concatenate(parts, axis=1)


def reduce_scatter_rows(halves, axis):
    size = lax.axis_size(axis)
    step = 1
    kept = [k.astype(jnp.float32) for k, _ in halves]
    sent = [t for _, t in halves]
    while True:
        perm = [(k, k ^ step) for k in range(size)]
        got = [lax.ppermute(t.astype(jnp.bfloat16), axis, perm) for t in sent]
        total = [k + g.astype(jnp.float32) for k, g in zip(kept, got)]
        step *= 2
        if step >= size:
            return total
        half = total[0].shape[0] // 2
        kept = [t[:half] for t in total]
        sent = [t[half:] for t in total]


def expert_kernel(recv_ref, w_in_ref, w_out_ref, pay_ref, hid_ref, q_ref):
    model = w_in_ref.shape[0]
    width = w_out_ref.shape[1]
    w_in = w_in_ref[...]
    w_out = w_out_ref[...]
    gate_up = jnp.dot(recv_ref[:, :model], w_in, preferred_element_type=jnp.float32)
    gate = gate_up[:, :width]
    upper = gate_up[:, width:]
    sigmoid_gate = 1.0 / (1.0 + jnp.exp(-gate))
    activated = gate * sigmoid_gate
    hidden = (activated * upper).astype(jnp.bfloat16)
    hid_ref[...] = hidden
    pay_ref[:, :model] = contract_cols(hidden, w_out).astype(jnp.bfloat16)
    grad_hidden = jnp.dot(recv_ref[:, model:], w_out, preferred_element_type=jnp.float32)
    grad_gate = grad_hidden * upper * sigmoid_gate * (1.0 + gate * (1.0 - sigmoid_gate))
    q_ref[:, :width] = grad_gate.astype(jnp.bfloat16)
    q_ref[:, width:] = (grad_hidden * activated).astype(jnp.bfloat16)
    pay_ref[:, model:] = contract_cols(q_ref[...], w_in).astype(jnp.bfloat16)


def expert_rows(recv, first, second):
    rows = recv.shape[0]
    model, width = second.shape
    vmem = pl.BlockSpec(memory_space=pltpu.VMEM)
    flops = 2 * rows * model * width * 6
    moved = 2 * (2 * rows * 2 * model + model * 3 * width + rows * 3 * width)
    return pl.pallas_call(
        expert_kernel,
        out_shape=(
            jax.ShapeDtypeStruct((rows, 2 * model), jnp.bfloat16),
            jax.ShapeDtypeStruct((rows, width), jnp.bfloat16),
            jax.ShapeDtypeStruct((rows, 2 * width), jnp.bfloat16),
        ),
        in_specs=[vmem, vmem, vmem],
        out_specs=(vmem, vmem, vmem),
        cost_estimate=pl.CostEstimate(
            flops=flops, bytes_accessed=moved, transcendentals=rows * width),
    )(recv, first, second)


def per_device(tokens, routes, route_weight, w_in, w_out, out_grad):
    token_count, model = tokens.shape
    experts = w_in.shape[0] * lax.axis_size("expert")
    capacity = 3 * token_count // (2 * experts)
    width = w_out.shape[2]
    replicas = lax.axis_size("dp")
    first = w_in[0]
    second = w_out[0]
    placer = placement_rows(routes, experts, capacity)
    cotangent = (route_weight * out_grad.astype(jnp.float32)).astype(jnp.bfloat16)
    both = jnp.concatenate([tokens, cotangent], axis=1)
    send = jnp.dot(placer, both, preferred_element_type=jnp.float32).astype(jnp.bfloat16)
    recv = lax.all_to_all(send, "expert", split_axis=0, concat_axis=0, tiled=True)
    payload, hidden, grad_both = expert_rows(recv, first, second)
    rows_in = recv[:, :model]
    rows_cot = recv[:, model:]
    back = lax.all_to_all(payload, "expert", split_axis=0, concat_axis=0, tiled=True)
    token_back = contract_rows(placer, back)
    mixed = (route_weight * token_back[:, :model]).astype(jnp.bfloat16)
    token_grad = token_back[:, model:].astype(jnp.bfloat16)
    halves = []
    for rows, right in ((rows_in, grad_both), (rows_cot, hidden)):
        ordered = halving_order(rows, "dp")
        middle = ordered.shape[1] // 2
        halves.append(tuple(
            contract_rows(piece, right).astype(jnp.bfloat16)
            for piece in (ordered[:, :middle], ordered[:, middle:])
        ))
    sum_first, sum_second = reduce_scatter_rows(halves, "dp")
    grad_in = (sum_first / replicas).astype(jnp.bfloat16)[None]
    grad_out = (sum_second / replicas).astype(jnp.bfloat16)[None]
    return (mixed, token_grad, grad_in, grad_out)


def solution(mesh):
    in_specs = (
        P(("expert", "dp"), None),
        P(("expert", "dp"), None),
        P(("expert", "dp"), None),
        P("expert", None, None),
        P("expert", None, None),
        P(("expert", "dp"), None),
    )
    out_specs = (
        P(("expert", "dp"), None),
        P(("expert", "dp"), None),
        P("expert", "dp", None),
        P("expert", "dp", None),
    )
    return jax.shard_map(
        per_device, mesh=mesh, in_specs=in_specs, out_specs=out_specs, check_vma=False
    )
```

```python
import jax
import jax.numpy as jnp
from jax import lax
from jax.experimental import pallas as pl
from jax.experimental.pallas import tpu as pltpu
from jax.sharding import PartitionSpec as P


def placement_rows(routes, experts, capacity):
    chosen = routes[:, 0]
    onehot = (chosen[:, None] == jnp.arange(experts, dtype=jnp.int32)[None, :]).astype(jnp.int32)
    ranks = jnp.sum(jnp.cumsum(onehot, axis=0) * onehot, axis=1) - 1
    target = chosen * capacity + ranks
    slots = jnp.arange(experts * capacity, dtype=jnp.int32)
    return (slots[:, None] == target[None, :]).astype(jnp.bfloat16)


def contract_rows(left, right):
    return lax.dot_general(
        left, right, (((0,), (0,)), ((), ())), preferred_element_type=jnp.float32
    )


def contract_cols(left, right):
    return lax.dot_general(
        left, right, (((1,), (1,)), ((), ())), preferred_element_type=jnp.float32
    )


def halving_order(rows, axis):
    size = lax.axis_size(axis)
    me = lax.axis_index(axis)
    bits = size.bit_length() - 1
    share = rows.shape[1] // size
    parts = []
    for p in range(size):
        rev = int(format(p, "0{}b".format(bits))[::-1], 2) if bits else 0
        start = (me ^ rev) * share
        parts.append(lax.dynamic_slice_in_dim(rows, start, share, axis=1))
    return jnp.concatenate(parts, axis=1)


def reduce_scatter_rows(halves, axis):
    size = lax.axis_size(axis)
    step = 1
    kept = [k.astype(jnp.float32) for k, _ in halves]
    sent = [t for _, t in halves]
    while True:
        perm = [(k, k ^ step) for k in range(size)]
        got = [lax.ppermute(t.astype(jnp.bfloat16), axis, perm) for t in sent]
        total = [k + g.astype(jnp.float32) for k, g in zip(kept, got)]
        step *= 2
        if step >= size:
            return total
        half = total[0].shape[0] // 2
        kept = [t[:half] for t in total]
        sent = [t[half:] for t in total]


def expert_kernel(recv_ref, w_in_ref, w_out_ref, pay_ref, hid_ref, q_ref):
    model = w_in_ref.shape[0]
    width = w_out_ref.shape[1]
    w_in = w_in_ref[...]
    w_out = w_out_ref[...]
    gate_up = jnp.dot(recv_ref[:, :model], w_in, preferred_element_type=jnp.float32)
    gate = gate_up[:, :width]
    upper = gate_up[:, width:]
    sigmoid_gate = 1.0 / (1.0 + jnp.exp(-gate))
    activated = gate * sigmoid_gate
    hidden = (activated * upper).astype(jnp.bfloat16)
    hid_ref[...] = hidden
    pay_ref[:, :model] = contract_cols(hidden, w_out).astype(jnp.bfloat16)
    grad_hidden = jnp.dot(recv_ref[:, model:], w_out, preferred_element_type=jnp.float32)
    grad_gate = grad_hidden * upper * sigmoid_gate * (1.0 + gate * (1.0 - sigmoid_gate))
    q_ref[:, :width] = grad_gate.astype(jnp.bfloat16)
    q_ref[:, width:] = (grad_hidden * activated).astype(jnp.bfloat16)
    pay_ref[:, model:] = contract_cols(q_ref[...], w_in).astype(jnp.bfloat16)


def expert_rows(recv, first, second):
    rows = recv.shape[0]
    model, width = second.shape
    vmem = pl.BlockSpec(memory_space=pltpu.VMEM)
    flops = 2 * rows * model * width * 6
    moved = 2 * (2 * rows * 2 * model + model * 3 * width + rows * 3 * width)
    return pl.pallas_call(
        expert_kernel,
        out_shape=(
            jax.ShapeDtypeStruct((rows, 2 * model), jnp.bfloat16),
            jax.ShapeDtypeStruct((rows, width), jnp.bfloat16),
            jax.ShapeDtypeStruct((rows, 2 * width), jnp.bfloat16),
        ),
        in_specs=[vmem, vmem, vmem],
        out_specs=(vmem, vmem, vmem),
        compiler_params=pltpu.CompilerParams(vmem_limit_bytes=16 * 1024 * 1024),
        cost_estimate=pl.CostEstimate(
            flops=flops, bytes_accessed=moved, transcendentals=rows * width),
    )(*[pltpu.with_memory_space_constraint(x, pltpu.VMEM) for x in (recv, first, second)])


def per_device(tokens, routes, route_weight, w_in, w_out, out_grad):
    token_count, model = tokens.shape
    experts = w_in.shape[0] * lax.axis_size("expert")
    capacity = 3 * token_count // (2 * experts)
    width = w_out.shape[2]
    replicas = lax.axis_size("dp")
    first = w_in[0]
    second = w_out[0]
    placer = placement_rows(routes, experts, capacity)
    cotangent = (route_weight * out_grad.astype(jnp.float32)).astype(jnp.bfloat16)
    both = jnp.concatenate([tokens, cotangent], axis=1)
    send = jnp.dot(placer, both, preferred_element_type=jnp.float32).astype(jnp.bfloat16)
    recv = lax.all_to_all(send, "expert", split_axis=0, concat_axis=0, tiled=True)
    payload, hidden, grad_both = expert_rows(recv, first, second)
    rows_in = recv[:, :model]
    rows_cot = recv[:, model:]
    back = lax.all_to_all(payload, "expert", split_axis=0, concat_axis=0, tiled=True)
    token_back = contract_rows(placer, back)
    mixed = (route_weight * token_back[:, :model]).astype(jnp.bfloat16)
    token_grad = token_back[:, model:].astype(jnp.bfloat16)
    halves = []
    for rows, right in ((rows_in, grad_both), (rows_cot, hidden)):
        ordered = halving_order(rows, "dp")
        middle = ordered.shape[1] // 2
        halves.append(tuple(
            contract_rows(piece, right).astype(jnp.bfloat16)
            for piece in (ordered[:, :middle], ordered[:, middle:])
        ))
    sum_first, sum_second = reduce_scatter_rows(halves, "dp")
    grad_in = (sum_first / replicas).astype(jnp.bfloat16)[None]
    grad_out = (sum_second / replicas).astype(jnp.bfloat16)[None]
    return (mixed, token_grad, grad_in, grad_out)


def solution(mesh):
    in_specs = (
        P(("expert", "dp"), None),
        P(("expert", "dp"), None),
        P(("expert", "dp"), None),
        P("expert", None, None),
        P("expert", None, None),
        P(("expert", "dp"), None),
    )
    out_specs = (
        P(("expert", "dp"), None),
        P(("expert", "dp"), None),
        P("expert", "dp", None),
        P("expert", "dp", None),
    )
    return jax.shard_map(
        per_device, mesh=mesh, in_specs=in_specs, out_specs=out_specs, check_vma=False
    )
```

```python
import jax
import jax.numpy as jnp
from jax import lax
from jax.experimental import pallas as pl
from jax.experimental.pallas import tpu as pltpu
from jax.sharding import PartitionSpec as P


def placement_rows(routes, experts, capacity):
    chosen = routes[:, 0]
    onehot = (chosen[:, None] == jnp.arange(experts, dtype=jnp.int32)[None, :]).astype(jnp.int32)
    ranks = jnp.sum(jnp.cumsum(onehot, axis=0) * onehot, axis=1) - 1
    target = chosen * capacity + ranks
    slots = jnp.arange(experts * capacity, dtype=jnp.int32)
    return (slots[:, None] == target[None, :]).astype(jnp.bfloat16)


def contract_rows(left, right):
    return lax.dot_general(
        left, right, (((0,), (0,)), ((), ())), preferred_element_type=jnp.float32
    )


def contract_cols(left, right):
    return lax.dot_general(
        left, right, (((1,), (1,)), ((), ())), preferred_element_type=jnp.float32
    )


def halving_order(rows, axis):
    size = lax.axis_size(axis)
    me = lax.axis_index(axis)
    bits = size.bit_length() - 1
    share = rows.shape[1] // size
    parts = []
    for p in range(size):
        rev = int(format(p, "0{}b".format(bits))[::-1], 2) if bits else 0
        start = (me ^ rev) * share
        parts.append(lax.dynamic_slice_in_dim(rows, start, share, axis=1))
    return jnp.concatenate(parts, axis=1)


def reduce_scatter_rows(halves, axis):
    size = lax.axis_size(axis)
    step = 1
    kept = [k.astype(jnp.float32) for k, _ in halves]
    sent = [t for _, t in halves]
    while True:
        perm = [(k, k ^ step) for k in range(size)]
        got = [lax.ppermute(t.astype(jnp.bfloat16), axis, perm) for t in sent]
        total = [k + g.astype(jnp.float32) for k, g in zip(kept, got)]
        step *= 2
        if step >= size:
            return total
        half = total[0].shape[0] // 2
        kept = [t[:half] for t in total]
        sent = [t[half:] for t in total]


def expert_kernel(recv_ref, w_in_hbm, w_out_hbm, pay_ref, hid_ref, q_ref,
                  w_in_ref, w_out_ref, sems):
    model = w_in_ref.shape[0]
    width = w_out_ref.shape[1]
    chunks = sems.shape[0] - 1
    depth = model // chunks
    loads = [
        pltpu.make_async_copy(
            w_in_hbm.at[pl.ds(c * depth, depth)], w_in_ref.at[pl.ds(c * depth, depth)], sems.at[c])
        for c in range(chunks)
    ]
    w_out_load = pltpu.make_async_copy(w_out_hbm, w_out_ref, sems.at[chunks])
    for load in loads:
        load.start()
    w_out_load.start()
    gate_up = None
    for c, load in enumerate(loads):
        load.wait()
        band = pl.ds(c * depth, depth)
        part = jnp.dot(recv_ref[:, band], w_in_ref[band, :], preferred_element_type=jnp.float32)
        gate_up = part if gate_up is None else gate_up + part
    w_out_load.wait()
    w_in = w_in_ref[...]
    w_out = w_out_ref[...]
    gate = gate_up[:, :width]
    upper = gate_up[:, width:]
    sigmoid_gate = 1.0 / (1.0 + jnp.exp(-gate))
    activated = gate * sigmoid_gate
    hidden = (activated * upper).astype(jnp.bfloat16)
    hid_ref[...] = hidden
    pay_ref[:, :model] = contract_cols(hidden, w_out).astype(jnp.bfloat16)
    grad_hidden = jnp.dot(recv_ref[:, model:], w_out, preferred_element_type=jnp.float32)
    grad_gate = grad_hidden * upper * sigmoid_gate * (1.0 + gate * (1.0 - sigmoid_gate))
    q_ref[:, :width] = grad_gate.astype(jnp.bfloat16)
    q_ref[:, width:] = (grad_hidden * activated).astype(jnp.bfloat16)
    pay_ref[:, model:] = contract_cols(q_ref[...], w_in).astype(jnp.bfloat16)


def expert_rows(recv, first, second):
    rows = recv.shape[0]
    model, width = second.shape
    chunks = 4 if model % 64 == 0 else 1
    vmem = pl.BlockSpec(memory_space=pltpu.VMEM)
    hbm = pl.BlockSpec(memory_space=pl.ANY)
    flops = 2 * rows * model * width * 6
    moved = 2 * (2 * rows * 2 * model + model * 3 * width + rows * 3 * width)
    return pl.pallas_call(
        expert_kernel,
        out_shape=(
            jax.ShapeDtypeStruct((rows, 2 * model), jnp.bfloat16),
            jax.ShapeDtypeStruct((rows, width), jnp.bfloat16),
            jax.ShapeDtypeStruct((rows, 2 * width), jnp.bfloat16),
        ),
        in_specs=[vmem, hbm, hbm],
        out_specs=(vmem, vmem, vmem),
        scratch_shapes=[
            pltpu.VMEM(first.shape, first.dtype),
            pltpu.VMEM(second.shape, second.dtype),
            pltpu.SemaphoreType.DMA((chunks + 1,)),
        ],
        compiler_params=pltpu.CompilerParams(vmem_limit_bytes=24 * 1024 * 1024),
        cost_estimate=pl.CostEstimate(
            flops=flops, bytes_accessed=moved, transcendentals=rows * width),
    )(
        pltpu.with_memory_space_constraint(recv, pltpu.VMEM),
        pltpu.with_memory_space_constraint(first, pltpu.HBM),
        pltpu.with_memory_space_constraint(second, pltpu.HBM),
    )


def per_device(tokens, routes, route_weight, w_in, w_out, out_grad):
    token_count, model = tokens.shape
    experts = w_in.shape[0] * lax.axis_size("expert")
    capacity = 3 * token_count // (2 * experts)
    width = w_out.shape[2]
    replicas = lax.axis_size("dp")
    first = w_in[0]
    second = w_out[0]
    placer = placement_rows(routes, experts, capacity)
    cotangent = (route_weight * out_grad.astype(jnp.float32)).astype(jnp.bfloat16)
    both = jnp.concatenate([tokens, cotangent], axis=1)
    send = jnp.dot(placer, both, preferred_element_type=jnp.float32).astype(jnp.bfloat16)
    recv = lax.all_to_all(send, "expert", split_axis=0, concat_axis=0, tiled=True)
    payload, hidden, grad_both = expert_rows(recv, first, second)
    rows_in = recv[:, :model]
    rows_cot = recv[:, model:]
    back = lax.all_to_all(payload, "expert", split_axis=0, concat_axis=0, tiled=True)
    token_back = contract_rows(placer, back)
    mixed = (route_weight * token_back[:, :model]).astype(jnp.bfloat16)
    token_grad = token_back[:, model:].astype(jnp.bfloat16)
    halves = []
    for rows, right in ((rows_in, grad_both), (rows_cot, hidden)):
        ordered = halving_order(rows, "dp")
        middle = ordered.shape[1] // 2
        halves.append(tuple(
            contract_rows(piece, right).astype(jnp.bfloat16)
            for piece in (ordered[:, :middle], ordered[:, middle:])
        ))
    sum_first, sum_second = reduce_scatter_rows(halves, "dp")
    grad_in = (sum_first / replicas).astype(jnp.bfloat16)[None]
    grad_out = (sum_second / replicas).astype(jnp.bfloat16)[None]
    return (mixed, token_grad, grad_in, grad_out)


def solution(mesh):
    in_specs = (
        P(("expert", "dp"), None),
        P(("expert", "dp"), None),
        P(("expert", "dp"), None),
        P("expert", None, None),
        P("expert", None, None),
        P(("expert", "dp"), None),
    )
    out_specs = (
        P(("expert", "dp"), None),
        P(("expert", "dp"), None),
        P("expert", "dp", None),
        P("expert", "dp", None),
    )
    return jax.shard_map(
        per_device, mesh=mesh, in_specs=in_specs, out_specs=out_specs, check_vma=False
    )
```

```python
import functools

import jax
import jax.numpy as jnp
from jax import lax
from jax.experimental import pallas as pl
from jax.experimental.pallas import tpu as pltpu
from jax.sharding import PartitionSpec as P


def placement_rows(routes, experts, capacity):
    chosen = routes[:, 0]
    onehot = (chosen[:, None] == jnp.arange(experts, dtype=jnp.int32)[None, :]).astype(jnp.int32)
    ranks = jnp.sum(jnp.cumsum(onehot, axis=0) * onehot, axis=1) - 1
    target = chosen * capacity + ranks
    slots = jnp.arange(experts * capacity, dtype=jnp.int32)
    return (slots[:, None] == target[None, :]).astype(jnp.bfloat16)


def contract_rows(left, right):
    return lax.dot_general(
        left, right, (((0,), (0,)), ((), ())), preferred_element_type=jnp.float32
    )


def contract_cols(left, right):
    return lax.dot_general(
        left, right, (((1,), (1,)), ((), ())), preferred_element_type=jnp.float32
    )


def halving_order(rows, axis):
    size = lax.axis_size(axis)
    me = lax.axis_index(axis)
    bits = size.bit_length() - 1
    share = rows.shape[1] // size
    parts = []
    for p in range(size):
        rev = int(format(p, "0{}b".format(bits))[::-1], 2) if bits else 0
        start = (me ^ rev) * share
        parts.append(lax.dynamic_slice_in_dim(rows, start, share, axis=1))
    return jnp.concatenate(parts, axis=1)


def reduce_scatter_rows(halves, axis):
    size = lax.axis_size(axis)
    step = 1
    kept = [k.astype(jnp.float32) for k, _ in halves]
    sent = [t for _, t in halves]
    while True:
        perm = [(k, k ^ step) for k in range(size)]
        got = [lax.ppermute(t.astype(jnp.bfloat16), axis, perm) for t in sent]
        total = [k + g.astype(jnp.float32) for k, g in zip(kept, got)]
        step *= 2
        if step >= size:
            return total
        half = total[0].shape[0] // 2
        kept = [t[:half] for t in total]
        sent = [t[half:] for t in total]


def expert_kernel(recv_ref, w_in_hbm, w_out_hbm, pay_ref, hid_ref, q_ref,
                  w_in_ref, w_out_ref, sems):
    model = w_in_ref.shape[0]
    width = w_out_ref.shape[1]
    chunks = sems.shape[0] - 1
    depth = model // chunks
    loads = [
        pltpu.make_async_copy(
            w_in_hbm.at[pl.ds(c * depth, depth)], w_in_ref.at[pl.ds(c * depth, depth)], sems.at[c])
        for c in range(chunks)
    ]
    w_out_load = pltpu.make_async_copy(w_out_hbm, w_out_ref, sems.at[chunks])
    for load in loads:
        load.start()
    w_out_load.start()
    gate_up = None
    for c, load in enumerate(loads):
        load.wait()
        band = pl.ds(c * depth, depth)
        part = jnp.dot(recv_ref[:, band], w_in_ref[band, :], preferred_element_type=jnp.float32)
        gate_up = part if gate_up is None else gate_up + part
    w_out_load.wait()
    w_in = w_in_ref[...]
    w_out = w_out_ref[...]
    gate = gate_up[:, :width]
    upper = gate_up[:, width:]
    sigmoid_gate = 1.0 / (1.0 + jnp.exp(-gate))
    activated = gate * sigmoid_gate
    hidden = (activated * upper).astype(jnp.bfloat16)
    hid_ref[...] = hidden
    pay_ref[:, :model] = contract_cols(hidden, w_out).astype(jnp.bfloat16)
    grad_hidden = jnp.dot(recv_ref[:, model:], w_out, preferred_element_type=jnp.float32)
    grad_gate = grad_hidden * upper * sigmoid_gate * (1.0 + gate * (1.0 - sigmoid_gate))
    q_ref[:, :width] = grad_gate.astype(jnp.bfloat16)
    q_ref[:, width:] = (grad_hidden * activated).astype(jnp.bfloat16)
    pay_ref[:, model:] = contract_cols(q_ref[...], w_in).astype(jnp.bfloat16)


def expert_rows(recv, first, second):
    rows = recv.shape[0]
    model, width = second.shape
    chunks = 4 if model % 64 == 0 else 1
    vmem = pl.BlockSpec(memory_space=pltpu.VMEM)
    hbm = pl.BlockSpec(memory_space=pl.ANY)
    flops = 2 * rows * model * width * 6
    moved = 2 * (2 * rows * 2 * model + model * 3 * width + rows * 3 * width)
    return pl.pallas_call(
        expert_kernel,
        out_shape=(
            jax.ShapeDtypeStruct((rows, 2 * model), jnp.bfloat16),
            jax.ShapeDtypeStruct((rows, width), jnp.bfloat16),
            jax.ShapeDtypeStruct((rows, 2 * width), jnp.bfloat16),
        ),
        in_specs=[vmem, hbm, hbm],
        out_specs=(vmem, vmem, vmem),
        scratch_shapes=[
            pltpu.VMEM(first.shape, first.dtype),
            pltpu.VMEM(second.shape, second.dtype),
            pltpu.SemaphoreType.DMA((chunks + 1,)),
        ],
        compiler_params=pltpu.CompilerParams(vmem_limit_bytes=24 * 1024 * 1024),
        cost_estimate=pl.CostEstimate(
            flops=flops, bytes_accessed=moved, transcendentals=rows * width),
    )(
        pltpu.with_memory_space_constraint(recv, pltpu.VMEM),
        pltpu.with_memory_space_constraint(first, pltpu.HBM),
        pltpu.with_memory_space_constraint(second, pltpu.HBM),
    )


def dispatch_kernel(experts, route_row_ref, weight_ref, tokens_ref, grad_ref, send_ref):
    slot_count, count = send_ref.shape[0], route_row_ref.shape[1]
    capacity = slot_count // experts
    model = tokens_ref.shape[1]
    chosen = route_row_ref[...]
    kinds = lax.broadcasted_iota(jnp.int32, (experts, count), 0)
    onehot = (chosen == kinds).astype(jnp.bfloat16)
    earlier = (lax.broadcasted_iota(jnp.int32, (count, count), 0)
               < lax.broadcasted_iota(jnp.int32, (count, count), 1)).astype(jnp.bfloat16)
    before = jnp.dot(onehot, earlier, preferred_element_type=jnp.float32)
    ranks = jnp.sum(before * onehot.astype(jnp.float32), axis=0, keepdims=True).astype(jnp.int32)
    target = chosen * capacity + ranks
    slots = lax.broadcasted_iota(jnp.int32, (slot_count, count), 0)
    placer = (slots == target).astype(jnp.bfloat16)
    cotangent = (weight_ref[...] * grad_ref[...].astype(jnp.float32)).astype(jnp.bfloat16)
    send_ref[:, :model] = jnp.dot(placer, tokens_ref[...], preferred_element_type=jnp.float32).astype(jnp.bfloat16)
    send_ref[:, model:] = jnp.dot(placer, cotangent, preferred_element_type=jnp.float32).astype(jnp.bfloat16)


def dispatch_rows(routes, route_weight, tokens, out_grad, experts, capacity):
    count, model = tokens.shape
    vmem = pl.BlockSpec(memory_space=pltpu.VMEM)
    return pl.pallas_call(
        functools.partial(dispatch_kernel, experts),
        out_shape=jax.ShapeDtypeStruct((experts * capacity, 2 * model), jnp.bfloat16),
        in_specs=[vmem] * 4,
        out_specs=vmem,
        compiler_params=pltpu.CompilerParams(vmem_limit_bytes=16 * 1024 * 1024),
        cost_estimate=pl.CostEstimate(
            flops=2 * experts * capacity * count * 2 * model,
            bytes_accessed=2 * (2 * count * model + experts * capacity * 2 * model),
            transcendentals=0),
    )(routes.reshape(1, count), route_weight, tokens, out_grad)


def per_device(tokens, routes, route_weight, w_in, w_out, out_grad):
    token_count, model = tokens.shape
    experts = w_in.shape[0] * lax.axis_size("expert")
    capacity = 3 * token_count // (2 * experts)
    width = w_out.shape[2]
    replicas = lax.axis_size("dp")
    first = w_in[0]
    second = w_out[0]
    placer = placement_rows(routes, experts, capacity)
    send = dispatch_rows(routes, route_weight, tokens, out_grad, experts, capacity)
    recv = lax.all_to_all(send, "expert", split_axis=0, concat_axis=0, tiled=True)
    payload, hidden, grad_both = expert_rows(recv, first, second)
    rows_in = recv[:, :model]
    rows_cot = recv[:, model:]
    back = lax.all_to_all(payload, "expert", split_axis=0, concat_axis=0, tiled=True)
    token_back = contract_rows(placer, back)
    mixed = (route_weight * token_back[:, :model]).astype(jnp.bfloat16)
    token_grad = token_back[:, model:].astype(jnp.bfloat16)
    halves = []
    for rows, right in ((rows_in, grad_both), (rows_cot, hidden)):
        ordered = halving_order(rows, "dp")
        middle = ordered.shape[1] // 2
        halves.append(tuple(
            contract_rows(piece, right).astype(jnp.bfloat16)
            for piece in (ordered[:, :middle], ordered[:, middle:])
        ))
    sum_first, sum_second = reduce_scatter_rows(halves, "dp")
    grad_in = (sum_first / replicas).astype(jnp.bfloat16)[None]
    grad_out = (sum_second / replicas).astype(jnp.bfloat16)[None]
    return (mixed, token_grad, grad_in, grad_out)


def solution(mesh):
    in_specs = (
        P(("expert", "dp"), None),
        P(("expert", "dp"), None),
        P(("expert", "dp"), None),
        P("expert", None, None),
        P("expert", None, None),
        P(("expert", "dp"), None),
    )
    out_specs = (
        P(("expert", "dp"), None),
        P(("expert", "dp"), None),
        P("expert", "dp", None),
        P("expert", "dp", None),
    )
    return jax.shard_map(
        per_device, mesh=mesh, in_specs=in_specs, out_specs=out_specs, check_vma=False
    )
```

```python
import functools

import jax
import jax.numpy as jnp
from jax import lax
from jax.experimental import pallas as pl
from jax.experimental.pallas import tpu as pltpu
from jax.sharding import PartitionSpec as P


def placement_rows(routes, experts, capacity):
    chosen = routes[:, 0]
    onehot = (chosen[:, None] == jnp.arange(experts, dtype=jnp.int32)[None, :]).astype(jnp.int32)
    ranks = jnp.sum(jnp.cumsum(onehot, axis=0) * onehot, axis=1) - 1
    target = chosen * capacity + ranks
    slots = jnp.arange(experts * capacity, dtype=jnp.int32)
    return (slots[:, None] == target[None, :]).astype(jnp.bfloat16)


def contract_rows(left, right):
    return lax.dot_general(
        left, right, (((0,), (0,)), ((), ())), preferred_element_type=jnp.float32
    )


def contract_cols(left, right):
    return lax.dot_general(
        left, right, (((1,), (1,)), ((), ())), preferred_element_type=jnp.float32
    )


def halving_order(rows, axis):
    size = lax.axis_size(axis)
    me = lax.axis_index(axis)
    bits = size.bit_length() - 1
    share = rows.shape[1] // size
    parts = []
    for p in range(size):
        rev = int(format(p, "0{}b".format(bits))[::-1], 2) if bits else 0
        start = (me ^ rev) * share
        parts.append(lax.dynamic_slice_in_dim(rows, start, share, axis=1))
    return jnp.concatenate(parts, axis=1)


def reduce_scatter_rows(halves, axis):
    size = lax.axis_size(axis)
    step = 1
    kept = [k.astype(jnp.float32) for k, _ in halves]
    sent = [t for _, t in halves]
    while True:
        perm = [(k, k ^ step) for k in range(size)]
        got = [lax.ppermute(t.astype(jnp.bfloat16), axis, perm) for t in sent]
        total = [k + g.astype(jnp.float32) for k, g in zip(kept, got)]
        step *= 2
        if step >= size:
            return total
        half = total[0].shape[0] // 2
        kept = [t[:half] for t in total]
        sent = [t[half:] for t in total]


def expert_kernel(recv_ref, w_in_hbm, w_out_hbm, pay_ref, hid_ref, q_ref,
                  w_in_ref, w_out_ref, sems):
    model = w_in_ref.shape[0]
    width = w_out_ref.shape[1]
    chunks = sems.shape[0] - 1
    depth = model // chunks
    loads = [
        pltpu.make_async_copy(
            w_in_hbm.at[pl.ds(c * depth, depth)], w_in_ref.at[pl.ds(c * depth, depth)], sems.at[c])
        for c in range(chunks)
    ]
    w_out_load = pltpu.make_async_copy(w_out_hbm, w_out_ref, sems.at[chunks])
    for load in loads:
        load.start()
    w_out_load.start()
    gate_up = None
    for c, load in enumerate(loads):
        load.wait()
        band = pl.ds(c * depth, depth)
        part = jnp.dot(recv_ref[:, band], w_in_ref[band, :], preferred_element_type=jnp.float32)
        gate_up = part if gate_up is None else gate_up + part
    w_out_load.wait()
    w_in = w_in_ref[...]
    w_out = w_out_ref[...]
    gate = gate_up[:, :width]
    upper = gate_up[:, width:]
    sigmoid_gate = 1.0 / (1.0 + jnp.exp(-gate))
    activated = gate * sigmoid_gate
    hidden = (activated * upper).astype(jnp.bfloat16)
    hid_ref[...] = hidden
    pay_ref[:, :model] = contract_cols(hidden, w_out).astype(jnp.bfloat16)
    grad_hidden = jnp.dot(recv_ref[:, model:], w_out, preferred_element_type=jnp.float32)
    grad_gate = grad_hidden * upper * sigmoid_gate * (1.0 + gate * (1.0 - sigmoid_gate))
    q_ref[:, :width] = grad_gate.astype(jnp.bfloat16)
    q_ref[:, width:] = (grad_hidden * activated).astype(jnp.bfloat16)
    pay_ref[:, model:] = contract_cols(q_ref[...], w_in).astype(jnp.bfloat16)


def expert_rows(recv, first, second):
    rows = recv.shape[0]
    model, width = second.shape
    chunks = 4 if model % 64 == 0 else 1
    vmem = pl.BlockSpec(memory_space=pltpu.VMEM)
    hbm = pl.BlockSpec(memory_space=pl.ANY)
    flops = 2 * rows * model * width * 6
    moved = 2 * (2 * rows * 2 * model + model * 3 * width + rows * 3 * width)
    return pl.pallas_call(
        expert_kernel,
        out_shape=(
            jax.ShapeDtypeStruct((rows, 2 * model), jnp.bfloat16),
            jax.ShapeDtypeStruct((rows, width), jnp.bfloat16),
            jax.ShapeDtypeStruct((rows, 2 * width), jnp.bfloat16),
        ),
        in_specs=[vmem, hbm, hbm],
        out_specs=(vmem, vmem, vmem),
        scratch_shapes=[
            pltpu.VMEM(first.shape, first.dtype),
            pltpu.VMEM(second.shape, second.dtype),
            pltpu.SemaphoreType.DMA((chunks + 1,)),
        ],
        compiler_params=pltpu.CompilerParams(vmem_limit_bytes=24 * 1024 * 1024),
        cost_estimate=pl.CostEstimate(
            flops=flops, bytes_accessed=moved, transcendentals=rows * width),
    )(
        pltpu.with_memory_space_constraint(recv, pltpu.VMEM),
        pltpu.with_memory_space_constraint(first, pltpu.HBM),
        pltpu.with_memory_space_constraint(second, pltpu.HBM),
    )


def dispatch_kernel(experts, route_row_ref, weight_ref, tokens_hbm, grad_hbm, send_ref,
                    tokens_ref, grad_ref, sems):
    loads = [
        pltpu.make_async_copy(tokens_hbm, tokens_ref, sems.at[0]),
        pltpu.make_async_copy(grad_hbm, grad_ref, sems.at[1]),
    ]
    for load in loads:
        load.start()
    slot_count, count = send_ref.shape[0], route_row_ref.shape[1]
    capacity = slot_count // experts
    model = tokens_ref.shape[1]
    chosen = route_row_ref[...]
    kinds = lax.broadcasted_iota(jnp.int32, (experts, count), 0)
    onehot = (chosen == kinds).astype(jnp.bfloat16)
    earlier = (lax.broadcasted_iota(jnp.int32, (count, count), 0)
               < lax.broadcasted_iota(jnp.int32, (count, count), 1)).astype(jnp.bfloat16)
    before = jnp.dot(onehot, earlier, preferred_element_type=jnp.float32)
    ranks = jnp.sum(before * onehot.astype(jnp.float32), axis=0, keepdims=True).astype(jnp.int32)
    target = chosen * capacity + ranks
    slots = lax.broadcasted_iota(jnp.int32, (slot_count, count), 0)
    placer = (slots == target).astype(jnp.bfloat16)
    loads[0].wait()
    send_ref[:, :model] = jnp.dot(placer, tokens_ref[...], preferred_element_type=jnp.float32).astype(jnp.bfloat16)
    loads[1].wait()
    cotangent = (weight_ref[...] * grad_ref[...].astype(jnp.float32)).astype(jnp.bfloat16)
    send_ref[:, model:] = jnp.dot(placer, cotangent, preferred_element_type=jnp.float32).astype(jnp.bfloat16)


def dispatch_rows(routes, route_weight, tokens, out_grad, experts, capacity):
    count, model = tokens.shape
    vmem = pl.BlockSpec(memory_space=pltpu.VMEM)
    hbm = pl.BlockSpec(memory_space=pl.ANY)
    return pl.pallas_call(
        functools.partial(dispatch_kernel, experts),
        out_shape=jax.ShapeDtypeStruct((experts * capacity, 2 * model), jnp.bfloat16),
        in_specs=[vmem, vmem, hbm, hbm],
        out_specs=vmem,
        scratch_shapes=[
            pltpu.VMEM(tokens.shape, tokens.dtype),
            pltpu.VMEM(out_grad.shape, out_grad.dtype),
            pltpu.SemaphoreType.DMA((2,)),
        ],
        compiler_params=pltpu.CompilerParams(vmem_limit_bytes=16 * 1024 * 1024),
        cost_estimate=pl.CostEstimate(
            flops=2 * experts * capacity * count * 2 * model,
            bytes_accessed=2 * (2 * count * model + experts * capacity * 2 * model),
            transcendentals=0),
    )(
        routes.reshape(1, count), route_weight,
        pltpu.with_memory_space_constraint(tokens, pltpu.HBM),
        pltpu.with_memory_space_constraint(out_grad, pltpu.HBM),
    )


def per_device(tokens, routes, route_weight, w_in, w_out, out_grad):
    token_count, model = tokens.shape
    experts = w_in.shape[0] * lax.axis_size("expert")
    capacity = 3 * token_count // (2 * experts)
    width = w_out.shape[2]
    replicas = lax.axis_size("dp")
    first = w_in[0]
    second = w_out[0]
    placer = placement_rows(routes, experts, capacity)
    send = dispatch_rows(routes, route_weight, tokens, out_grad, experts, capacity)
    recv = lax.all_to_all(send, "expert", split_axis=0, concat_axis=0, tiled=True)
    payload, hidden, grad_both = expert_rows(recv, first, second)
    rows_in = recv[:, :model]
    rows_cot = recv[:, model:]
    back = lax.all_to_all(payload, "expert", split_axis=0, concat_axis=0, tiled=True)
    token_back = contract_rows(placer, back)
    mixed = (route_weight * token_back[:, :model]).astype(jnp.bfloat16)
    token_grad = token_back[:, model:].astype(jnp.bfloat16)
    halves = []
    for rows, right in ((rows_in, grad_both), (rows_cot, hidden)):
        ordered = halving_order(rows, "dp")
        middle = ordered.shape[1] // 2
        halves.append(tuple(
            contract_rows(piece, right).astype(jnp.bfloat16)
            for piece in (ordered[:, :middle], ordered[:, middle:])
        ))
    sum_first, sum_second = reduce_scatter_rows(halves, "dp")
    grad_in = (sum_first / replicas).astype(jnp.bfloat16)[None]
    grad_out = (sum_second / replicas).astype(jnp.bfloat16)[None]
    return (mixed, token_grad, grad_in, grad_out)


def solution(mesh):
    in_specs = (
        P(("expert", "dp"), None),
        P(("expert", "dp"), None),
        P(("expert", "dp"), None),
        P("expert", None, None),
        P("expert", None, None),
        P(("expert", "dp"), None),
    )
    out_specs = (
        P(("expert", "dp"), None),
        P(("expert", "dp"), None),
        P("expert", "dp", None),
        P("expert", "dp", None),
    )
    return jax.shard_map(
        per_device, mesh=mesh, in_specs=in_specs, out_specs=out_specs, check_vma=False
    )
```

```python
import functools

import jax
import jax.numpy as jnp
from jax import lax
from jax.experimental import pallas as pl
from jax.experimental.pallas import tpu as pltpu
from jax.sharding import PartitionSpec as P


def contract_rows(left, right):
    return lax.dot_general(
        left, right, (((0,), (0,)), ((), ())), preferred_element_type=jnp.float32
    )


def contract_cols(left, right):
    return lax.dot_general(
        left, right, (((1,), (1,)), ((), ())), preferred_element_type=jnp.float32
    )


def halving_order(rows, axis):
    size = lax.axis_size(axis)
    me = lax.axis_index(axis)
    bits = size.bit_length() - 1
    share = rows.shape[1] // size
    parts = []
    for p in range(size):
        rev = int(format(p, "0{}b".format(bits))[::-1], 2) if bits else 0
        start = (me ^ rev) * share
        parts.append(lax.dynamic_slice_in_dim(rows, start, share, axis=1))
    return jnp.concatenate(parts, axis=1)


def reduce_scatter_rows(halves, axis):
    size = lax.axis_size(axis)
    step = 1
    kept = [k.astype(jnp.float32) for k, _ in halves]
    sent = [t for _, t in halves]
    while True:
        perm = [(k, k ^ step) for k in range(size)]
        got = [lax.ppermute(t.astype(jnp.bfloat16), axis, perm) for t in sent]
        total = [k + g.astype(jnp.float32) for k, g in zip(kept, got)]
        step *= 2
        if step >= size:
            return total
        half = total[0].shape[0] // 2
        kept = [t[:half] for t in total]
        sent = [t[half:] for t in total]


def expert_kernel(recv_ref, w_in_hbm, w_out_hbm, pay_ref, hid_ref, q_ref,
                  w_in_ref, w_out_ref, sems):
    model = w_in_ref.shape[0]
    width = w_out_ref.shape[1]
    chunks = sems.shape[0] - 1
    depth = model // chunks
    loads = [
        pltpu.make_async_copy(
            w_in_hbm.at[pl.ds(c * depth, depth)], w_in_ref.at[pl.ds(c * depth, depth)], sems.at[c])
        for c in range(chunks)
    ]
    w_out_load = pltpu.make_async_copy(w_out_hbm, w_out_ref, sems.at[chunks])
    for load in loads:
        load.start()
    w_out_load.start()
    gate_up = None
    for c, load in enumerate(loads):
        load.wait()
        band = pl.ds(c * depth, depth)
        part = jnp.dot(recv_ref[:, band], w_in_ref[band, :], preferred_element_type=jnp.float32)
        gate_up = part if gate_up is None else gate_up + part
    w_out_load.wait()
    w_in = w_in_ref[...]
    w_out = w_out_ref[...]
    gate = gate_up[:, :width]
    upper = gate_up[:, width:]
    sigmoid_gate = 1.0 / (1.0 + jnp.exp(-gate))
    activated = gate * sigmoid_gate
    hidden = (activated * upper).astype(jnp.bfloat16)
    hid_ref[...] = hidden
    pay_ref[:, :model] = contract_cols(hidden, w_out).astype(jnp.bfloat16)
    grad_hidden = jnp.dot(recv_ref[:, model:], w_out, preferred_element_type=jnp.float32)
    grad_gate = grad_hidden * upper * sigmoid_gate * (1.0 + gate * (1.0 - sigmoid_gate))
    q_ref[:, :width] = grad_gate.astype(jnp.bfloat16)
    q_ref[:, width:] = (grad_hidden * activated).astype(jnp.bfloat16)
    pay_ref[:, model:] = contract_cols(q_ref[...], w_in).astype(jnp.bfloat16)


def expert_rows(recv, first, second):
    rows = recv.shape[0]
    model, width = second.shape
    chunks = 4 if model % 64 == 0 else 1
    vmem = pl.BlockSpec(memory_space=pltpu.VMEM)
    hbm = pl.BlockSpec(memory_space=pl.ANY)
    flops = 2 * rows * model * width * 6
    moved = 2 * (2 * rows * 2 * model + model * 3 * width + rows * 3 * width)
    return pl.pallas_call(
        expert_kernel,
        out_shape=(
            jax.ShapeDtypeStruct((rows, 2 * model), jnp.bfloat16),
            jax.ShapeDtypeStruct((rows, width), jnp.bfloat16),
            jax.ShapeDtypeStruct((rows, 2 * width), jnp.bfloat16),
        ),
        in_specs=[vmem, hbm, hbm],
        out_specs=(vmem, vmem, vmem),
        scratch_shapes=[
            pltpu.VMEM(first.shape, first.dtype),
            pltpu.VMEM(second.shape, second.dtype),
            pltpu.SemaphoreType.DMA((chunks + 1,)),
        ],
        compiler_params=pltpu.CompilerParams(vmem_limit_bytes=24 * 1024 * 1024),
        cost_estimate=pl.CostEstimate(
            flops=flops, bytes_accessed=moved, transcendentals=rows * width),
    )(
        pltpu.with_memory_space_constraint(recv, pltpu.VMEM),
        pltpu.with_memory_space_constraint(first, pltpu.HBM),
        pltpu.with_memory_space_constraint(second, pltpu.HBM),
    )


def dispatch_kernel(experts, route_row_ref, weight_ref, tokens_hbm, grad_hbm, send_ref,
                    placer_ref, tokens_ref, grad_ref, sems):
    loads = [
        pltpu.make_async_copy(tokens_hbm, tokens_ref, sems.at[0]),
        pltpu.make_async_copy(grad_hbm, grad_ref, sems.at[1]),
    ]
    for load in loads:
        load.start()
    slot_count, count = send_ref.shape[0], route_row_ref.shape[1]
    capacity = slot_count // experts
    model = tokens_ref.shape[1]
    chosen = route_row_ref[...]
    kinds = lax.broadcasted_iota(jnp.int32, (experts, count), 0)
    onehot = (chosen == kinds).astype(jnp.bfloat16)
    earlier = (lax.broadcasted_iota(jnp.int32, (count, count), 0)
               < lax.broadcasted_iota(jnp.int32, (count, count), 1)).astype(jnp.bfloat16)
    before = jnp.dot(onehot, earlier, preferred_element_type=jnp.float32)
    ranks = jnp.sum(before * onehot.astype(jnp.float32), axis=0, keepdims=True).astype(jnp.int32)
    target = chosen * capacity + ranks
    slots = lax.broadcasted_iota(jnp.int32, (slot_count, count), 0)
    placer = (slots == target).astype(jnp.bfloat16)
    placer_ref[...] = placer
    loads[0].wait()
    send_ref[:, :model] = jnp.dot(placer, tokens_ref[...], preferred_element_type=jnp.float32).astype(jnp.bfloat16)
    loads[1].wait()
    cotangent = (weight_ref[...] * grad_ref[...].astype(jnp.float32)).astype(jnp.bfloat16)
    send_ref[:, model:] = jnp.dot(placer, cotangent, preferred_element_type=jnp.float32).astype(jnp.bfloat16)


def dispatch_rows(routes, route_weight, tokens, out_grad, experts, capacity):
    count, model = tokens.shape
    vmem = pl.BlockSpec(memory_space=pltpu.VMEM)
    hbm = pl.BlockSpec(memory_space=pl.ANY)
    return pl.pallas_call(
        functools.partial(dispatch_kernel, experts),
        out_shape=(
            jax.ShapeDtypeStruct((experts * capacity, 2 * model), jnp.bfloat16),
            jax.ShapeDtypeStruct((experts * capacity, count), jnp.bfloat16),
        ),
        in_specs=[vmem, vmem, hbm, hbm],
        out_specs=(vmem, vmem),
        scratch_shapes=[
            pltpu.VMEM(tokens.shape, tokens.dtype),
            pltpu.VMEM(out_grad.shape, out_grad.dtype),
            pltpu.SemaphoreType.DMA((2,)),
        ],
        compiler_params=pltpu.CompilerParams(vmem_limit_bytes=16 * 1024 * 1024),
        cost_estimate=pl.CostEstimate(
            flops=2 * experts * capacity * count * 2 * model,
            bytes_accessed=2 * (2 * count * model + experts * capacity * 2 * model),
            transcendentals=0),
    )(
        routes.reshape(1, count), route_weight,
        pltpu.with_memory_space_constraint(tokens, pltpu.HBM),
        pltpu.with_memory_space_constraint(out_grad, pltpu.HBM),
    )


def per_device(tokens, routes, route_weight, w_in, w_out, out_grad):
    token_count, model = tokens.shape
    experts = w_in.shape[0] * lax.axis_size("expert")
    capacity = 3 * token_count // (2 * experts)
    width = w_out.shape[2]
    replicas = lax.axis_size("dp")
    first = w_in[0]
    second = w_out[0]
    send, placer = dispatch_rows(routes, route_weight, tokens, out_grad, experts, capacity)
    recv = lax.all_to_all(send, "expert", split_axis=0, concat_axis=0, tiled=True)
    payload, hidden, grad_both = expert_rows(recv, first, second)
    rows_in = recv[:, :model]
    rows_cot = recv[:, model:]
    back = lax.all_to_all(payload, "expert", split_axis=0, concat_axis=0, tiled=True)
    token_back = contract_rows(placer, back)
    mixed = (route_weight * token_back[:, :model]).astype(jnp.bfloat16)
    token_grad = token_back[:, model:].astype(jnp.bfloat16)
    halves = []
    for rows, right in ((rows_in, grad_both), (rows_cot, hidden)):
        ordered = halving_order(rows, "dp")
        middle = ordered.shape[1] // 2
        halves.append(tuple(
            contract_rows(piece, right).astype(jnp.bfloat16)
            for piece in (ordered[:, :middle], ordered[:, middle:])
        ))
    sum_first, sum_second = reduce_scatter_rows(halves, "dp")
    grad_in = (sum_first / replicas).astype(jnp.bfloat16)[None]
    grad_out = (sum_second / replicas).astype(jnp.bfloat16)[None]
    return (mixed, token_grad, grad_in, grad_out)


def solution(mesh):
    in_specs = (
        P(("expert", "dp"), None),
        P(("expert", "dp"), None),
        P(("expert", "dp"), None),
        P("expert", None, None),
        P("expert", None, None),
        P(("expert", "dp"), None),
    )
    out_specs = (
        P(("expert", "dp"), None),
        P(("expert", "dp"), None),
        P("expert", "dp", None),
        P("expert", "dp", None),
    )
    return jax.shard_map(
        per_device, mesh=mesh, in_specs=in_specs, out_specs=out_specs, check_vma=False
    )
```

```python
import functools

import jax
import jax.numpy as jnp
from jax import lax
from jax.experimental import pallas as pl
from jax.experimental.pallas import tpu as pltpu
from jax.sharding import PartitionSpec as P


def contract_rows(left, right):
    return lax.dot_general(
        left, right, (((0,), (0,)), ((), ())), preferred_element_type=jnp.float32
    )


def contract_cols(left, right):
    return lax.dot_general(
        left, right, (((1,), (1,)), ((), ())), preferred_element_type=jnp.float32
    )


def halving_order(rows, axis):
    size = lax.axis_size(axis)
    me = lax.axis_index(axis)
    bits = size.bit_length() - 1
    share = rows.shape[1] // size
    parts = []
    for p in range(size):
        rev = int(format(p, "0{}b".format(bits))[::-1], 2) if bits else 0
        start = (me ^ rev) * share
        parts.append(lax.dynamic_slice_in_dim(rows, start, share, axis=1))
    return jnp.concatenate(parts, axis=1)


def reduce_scatter_rows(halves, axis):
    size = lax.axis_size(axis)
    step = 1
    kept = [k.astype(jnp.float32) for k, _ in halves]
    sent = [t for _, t in halves]
    while True:
        perm = [(k, k ^ step) for k in range(size)]
        got = [lax.ppermute(t.astype(jnp.bfloat16), axis, perm) for t in sent]
        total = [k + g.astype(jnp.float32) for k, g in zip(kept, got)]
        step *= 2
        if step >= size:
            return total
        half = total[0].shape[0] // 2
        kept = [t[:half] for t in total]
        sent = [t[half:] for t in total]


def expert_kernel(recv_ref, w_in_hbm, w_out_hbm, pay_ref, hid_ref, q_ref,
                  w_in_ref, w_out_ref, sems):
    model = w_in_ref.shape[0]
    width = w_out_ref.shape[1]
    chunks = sems.shape[0] - 1
    depth = model // chunks
    loads = [
        pltpu.make_async_copy(
            w_in_hbm.at[pl.ds(c * depth, depth)], w_in_ref.at[pl.ds(c * depth, depth)], sems.at[c])
        for c in range(chunks)
    ]
    w_out_load = pltpu.make_async_copy(w_out_hbm, w_out_ref, sems.at[chunks])
    for load in loads:
        load.start()
    w_out_load.start()
    gate_up = None
    for c, load in enumerate(loads):
        load.wait()
        band = pl.ds(c * depth, depth)
        part = jnp.dot(recv_ref[:, band], w_in_ref[band, :], preferred_element_type=jnp.float32)
        gate_up = part if gate_up is None else gate_up + part
    w_out_load.wait()
    w_in = w_in_ref[...]
    w_out = w_out_ref[...]
    gate = gate_up[:, :width]
    upper = gate_up[:, width:]
    sigmoid_gate = 1.0 / (1.0 + jnp.exp(-gate))
    activated = gate * sigmoid_gate
    hidden = (activated * upper).astype(jnp.bfloat16)
    hid_ref[...] = hidden
    pay_ref[:, :model] = contract_cols(hidden, w_out).astype(jnp.bfloat16)
    grad_hidden = jnp.dot(recv_ref[:, model:], w_out, preferred_element_type=jnp.float32)
    grad_gate = grad_hidden * upper * sigmoid_gate * (1.0 + gate * (1.0 - sigmoid_gate))
    q_ref[:, :width] = grad_gate.astype(jnp.bfloat16)
    q_ref[:, width:] = (grad_hidden * activated).astype(jnp.bfloat16)
    pay_ref[:, model:] = contract_cols(q_ref[...], w_in).astype(jnp.bfloat16)


def expert_rows(recv, first, second):
    rows = recv.shape[0]
    model, width = second.shape
    chunks = 4 if model % 64 == 0 else 1
    vmem = pl.BlockSpec(memory_space=pltpu.VMEM)
    hbm = pl.BlockSpec(memory_space=pl.ANY)
    flops = 2 * rows * model * width * 6
    moved = 2 * (2 * rows * 2 * model + model * 3 * width + rows * 3 * width)
    return pl.pallas_call(
        expert_kernel,
        out_shape=(
            jax.ShapeDtypeStruct((rows, 2 * model), jnp.bfloat16),
            jax.ShapeDtypeStruct((rows, width), jnp.bfloat16),
            jax.ShapeDtypeStruct((rows, 2 * width), jnp.bfloat16),
        ),
        in_specs=[vmem, hbm, hbm],
        out_specs=(vmem, vmem, vmem),
        scratch_shapes=[
            pltpu.VMEM(first.shape, first.dtype),
            pltpu.VMEM(second.shape, second.dtype),
            pltpu.SemaphoreType.DMA((chunks + 1,)),
        ],
        compiler_params=pltpu.CompilerParams(vmem_limit_bytes=24 * 1024 * 1024),
        cost_estimate=pl.CostEstimate(
            flops=flops, bytes_accessed=moved, transcendentals=rows * width),
    )(
        pltpu.with_memory_space_constraint(recv, pltpu.VMEM),
        pltpu.with_memory_space_constraint(first, pltpu.HBM),
        pltpu.with_memory_space_constraint(second, pltpu.HBM),
    )


def dispatch_kernel(experts, route_row_ref, weight_ref, tokens_hbm, grad_hbm, send_ref,
                    placer_ref, gather_ref, tokens_ref, grad_ref, sems):
    loads = [
        pltpu.make_async_copy(tokens_hbm, tokens_ref, sems.at[0]),
        pltpu.make_async_copy(grad_hbm, grad_ref, sems.at[1]),
    ]
    for load in loads:
        load.start()
    slot_count, count = send_ref.shape[0], route_row_ref.shape[1]
    capacity = slot_count // experts
    model = tokens_ref.shape[1]
    chosen = route_row_ref[...]
    kinds = lax.broadcasted_iota(jnp.int32, (experts, count), 0)
    onehot = (chosen == kinds).astype(jnp.bfloat16)
    earlier = (lax.broadcasted_iota(jnp.int32, (count, count), 0)
               < lax.broadcasted_iota(jnp.int32, (count, count), 1)).astype(jnp.bfloat16)
    before = jnp.dot(onehot, earlier, preferred_element_type=jnp.float32)
    ranks = jnp.sum(before * onehot.astype(jnp.float32), axis=0, keepdims=True).astype(jnp.int32)
    target = chosen * capacity + ranks
    slots = lax.broadcasted_iota(jnp.int32, (slot_count, count), 0)
    placer = (slots == target).astype(jnp.bfloat16)
    placer_ref[...] = placer
    gather_ref[...] = jnp.transpose(placer)
    loads[0].wait()
    send_ref[:, :model] = jnp.dot(placer, tokens_ref[...], preferred_element_type=jnp.float32).astype(jnp.bfloat16)
    loads[1].wait()
    cotangent = (weight_ref[...] * grad_ref[...].astype(jnp.float32)).astype(jnp.bfloat16)
    send_ref[:, model:] = jnp.dot(placer, cotangent, preferred_element_type=jnp.float32).astype(jnp.bfloat16)


def dispatch_rows(routes, route_weight, tokens, out_grad, experts, capacity):
    count, model = tokens.shape
    vmem = pl.BlockSpec(memory_space=pltpu.VMEM)
    hbm = pl.BlockSpec(memory_space=pl.ANY)
    return pl.pallas_call(
        functools.partial(dispatch_kernel, experts),
        out_shape=(
            jax.ShapeDtypeStruct((experts * capacity, 2 * model), jnp.bfloat16),
            jax.ShapeDtypeStruct((experts * capacity, count), jnp.bfloat16),
            jax.ShapeDtypeStruct((count, experts * capacity), jnp.bfloat16),
        ),
        in_specs=[vmem, vmem, hbm, hbm],
        out_specs=(vmem, vmem, vmem),
        scratch_shapes=[
            pltpu.VMEM(tokens.shape, tokens.dtype),
            pltpu.VMEM(out_grad.shape, out_grad.dtype),
            pltpu.SemaphoreType.DMA((2,)),
        ],
        compiler_params=pltpu.CompilerParams(vmem_limit_bytes=16 * 1024 * 1024),
        cost_estimate=pl.CostEstimate(
            flops=2 * experts * capacity * count * 2 * model,
            bytes_accessed=2 * (2 * count * model + experts * capacity * 2 * model),
            transcendentals=0),
    )(
        routes.reshape(1, count), route_weight,
        pltpu.with_memory_space_constraint(tokens, pltpu.HBM),
        pltpu.with_memory_space_constraint(out_grad, pltpu.HBM),
    )


def combine_kernel(back_ref, gather_ref, weight_ref, mixed_ref, grad_ref):
    model = mixed_ref.shape[1]
    gather = gather_ref[...]
    mixed_ref[...] = (weight_ref[...] * jnp.dot(
        gather, back_ref[:, :model], preferred_element_type=jnp.float32)).astype(jnp.bfloat16)
    grad_ref[...] = jnp.dot(
        gather, back_ref[:, model:], preferred_element_type=jnp.float32).astype(jnp.bfloat16)


def combine_rows(back, gather, route_weight):
    count, slot_count = gather.shape
    model = back.shape[1] // 2
    vmem = pl.BlockSpec(memory_space=pltpu.VMEM)
    return pl.pallas_call(
        combine_kernel,
        out_shape=(
            jax.ShapeDtypeStruct((count, model), jnp.bfloat16),
            jax.ShapeDtypeStruct((count, model), jnp.bfloat16),
        ),
        in_specs=[vmem] * 3,
        out_specs=(vmem, vmem),
        compiler_params=pltpu.CompilerParams(vmem_limit_bytes=16 * 1024 * 1024),
        cost_estimate=pl.CostEstimate(
            flops=2 * count * slot_count * 2 * model,
            bytes_accessed=2 * (slot_count * 2 * model + 2 * count * model),
            transcendentals=0),
    )(pltpu.with_memory_space_constraint(back, pltpu.VMEM), gather, route_weight)


def per_device(tokens, routes, route_weight, w_in, w_out, out_grad):
    token_count, model = tokens.shape
    experts = w_in.shape[0] * lax.axis_size("expert")
    capacity = 3 * token_count // (2 * experts)
    width = w_out.shape[2]
    replicas = lax.axis_size("dp")
    first = w_in[0]
    second = w_out[0]
    send, placer, gather = dispatch_rows(routes, route_weight, tokens, out_grad, experts, capacity)
    recv = lax.all_to_all(send, "expert", split_axis=0, concat_axis=0, tiled=True)
    payload, hidden, grad_both = expert_rows(recv, first, second)
    rows_in = recv[:, :model]
    rows_cot = recv[:, model:]
    back = lax.all_to_all(payload, "expert", split_axis=0, concat_axis=0, tiled=True)
    mixed, token_grad = combine_rows(back, gather, route_weight)
    halves = []
    for rows, right in ((rows_in, grad_both), (rows_cot, hidden)):
        ordered = halving_order(rows, "dp")
        middle = ordered.shape[1] // 2
        halves.append(tuple(
            contract_rows(piece, right).astype(jnp.bfloat16)
            for piece in (ordered[:, :middle], ordered[:, middle:])
        ))
    sum_first, sum_second = reduce_scatter_rows(halves, "dp")
    grad_in = (sum_first / replicas).astype(jnp.bfloat16)[None]
    grad_out = (sum_second / replicas).astype(jnp.bfloat16)[None]
    return (mixed, token_grad, grad_in, grad_out)


def solution(mesh):
    in_specs = (
        P(("expert", "dp"), None),
        P(("expert", "dp"), None),
        P(("expert", "dp"), None),
        P("expert", None, None),
        P("expert", None, None),
        P(("expert", "dp"), None),
    )
    out_specs = (
        P(("expert", "dp"), None),
        P(("expert", "dp"), None),
        P("expert", "dp", None),
        P("expert", "dp", None),
    )
    return jax.shard_map(
        per_device, mesh=mesh, in_specs=in_specs, out_specs=out_specs, check_vma=False
    )
```

```python
import functools

import jax
import jax.numpy as jnp
from jax import lax
from jax.experimental import pallas as pl
from jax.experimental.pallas import tpu as pltpu
from jax.sharding import PartitionSpec as P


def contract_rows(left, right):
    return lax.dot_general(
        left, right, (((0,), (0,)), ((), ())), preferred_element_type=jnp.float32
    )


def contract_cols(left, right):
    return lax.dot_general(
        left, right, (((1,), (1,)), ((), ())), preferred_element_type=jnp.float32
    )


def halving_order(rows, axis):
    size = lax.axis_size(axis)
    me = lax.axis_index(axis)
    bits = size.bit_length() - 1
    share = rows.shape[1] // size
    parts = []
    for p in range(size):
        rev = int(format(p, "0{}b".format(bits))[::-1], 2) if bits else 0
        start = (me ^ rev) * share
        parts.append(lax.dynamic_slice_in_dim(rows, start, share, axis=1))
    return jnp.concatenate(parts, axis=1)


def reduce_scatter_rows(halves, axis):
    size = lax.axis_size(axis)
    step = 1
    kept = [k.astype(jnp.float32) for k, _ in halves]
    sent = [t for _, t in halves]
    while True:
        perm = [(k, k ^ step) for k in range(size)]
        got = [lax.ppermute(t.astype(jnp.bfloat16), axis, perm) for t in sent]
        total = [k + g.astype(jnp.float32) for k, g in zip(kept, got)]
        step *= 2
        if step >= size:
            return total
        half = total[0].shape[0] // 2
        kept = [t[:half] for t in total]
        sent = [t[half:] for t in total]


def expert_kernel(recv_ref, w_in_hbm, w_out_hbm, pay_ref, hid_ref, q_ref,
                  w_in_ref, w_out_ref, sems):
    model = w_in_ref.shape[0]
    width = w_out_ref.shape[1]
    chunks = sems.shape[0] - 1
    depth = model // chunks
    loads = [
        pltpu.make_async_copy(
            w_in_hbm.at[pl.ds(c * depth, depth)], w_in_ref.at[pl.ds(c * depth, depth)], sems.at[c])
        for c in range(chunks)
    ]
    w_out_load = pltpu.make_async_copy(w_out_hbm, w_out_ref, sems.at[chunks])
    for load in loads:
        load.start()
    w_out_load.start()
    gate_up = None
    for c, load in enumerate(loads):
        load.wait()
        band = pl.ds(c * depth, depth)
        part = jnp.dot(recv_ref[:, band], w_in_ref[band, :], preferred_element_type=jnp.float32)
        gate_up = part if gate_up is None else gate_up + part
    w_out_load.wait()
    w_in = w_in_ref[...]
    w_out = w_out_ref[...]
    gate = gate_up[:, :width]
    upper = gate_up[:, width:]
    sigmoid_gate = 1.0 / (1.0 + jnp.exp(-gate))
    activated = gate * sigmoid_gate
    hidden = (activated * upper).astype(jnp.bfloat16)
    hid_ref[...] = hidden
    pay_ref[:, :model] = contract_cols(hidden, w_out).astype(jnp.bfloat16)
    grad_hidden = jnp.dot(recv_ref[:, model:], w_out, preferred_element_type=jnp.float32)
    grad_gate = grad_hidden * upper * sigmoid_gate * (1.0 + gate * (1.0 - sigmoid_gate))
    q_ref[:, :width] = grad_gate.astype(jnp.bfloat16)
    q_ref[:, width:] = (grad_hidden * activated).astype(jnp.bfloat16)
    pay_ref[:, model:] = contract_cols(q_ref[...], w_in).astype(jnp.bfloat16)


def expert_rows(recv, first, second):
    rows = recv.shape[0]
    model, width = second.shape
    chunks = 4 if model % 64 == 0 else 1
    vmem = pl.BlockSpec(memory_space=pltpu.VMEM)
    hbm = pl.BlockSpec(memory_space=pl.ANY)
    flops = 2 * rows * model * width * 6
    moved = 2 * (2 * rows * 2 * model + model * 3 * width + rows * 3 * width)
    return pl.pallas_call(
        expert_kernel,
        out_shape=(
            jax.ShapeDtypeStruct((rows, 2 * model), jnp.bfloat16),
            jax.ShapeDtypeStruct((rows, width), jnp.bfloat16),
            jax.ShapeDtypeStruct((rows, 2 * width), jnp.bfloat16),
        ),
        in_specs=[vmem, hbm, hbm],
        out_specs=(vmem, vmem, vmem),
        scratch_shapes=[
            pltpu.VMEM(first.shape, first.dtype),
            pltpu.VMEM(second.shape, second.dtype),
            pltpu.SemaphoreType.DMA((chunks + 1,)),
        ],
        compiler_params=pltpu.CompilerParams(vmem_limit_bytes=24 * 1024 * 1024),
        cost_estimate=pl.CostEstimate(
            flops=flops, bytes_accessed=moved, transcendentals=rows * width),
    )(
        pltpu.with_memory_space_constraint(recv, pltpu.VMEM),
        pltpu.with_memory_space_constraint(first, pltpu.HBM),
        pltpu.with_memory_space_constraint(second, pltpu.HBM),
    )


def dispatch_kernel(experts, route_hbm, weight_hbm, tokens_hbm, grad_hbm, send_ref,
                    placer_ref, gather_ref, column_ref, route_row_ref, weight_row_ref,
                    tokens_ref, grad_ref, sems):
    rows_in = [
        pltpu.make_async_copy(route_hbm, route_row_ref, sems.at[2]),
        pltpu.make_async_copy(weight_hbm, weight_row_ref, sems.at[3]),
    ]
    loads = [
        pltpu.make_async_copy(tokens_hbm, tokens_ref, sems.at[0]),
        pltpu.make_async_copy(grad_hbm, grad_ref, sems.at[1]),
    ]
    for load in rows_in + loads:
        load.start()
    for load in rows_in:
        load.wait()
    slot_count, count = send_ref.shape[0], route_row_ref.shape[1]
    capacity = slot_count // experts
    model = tokens_ref.shape[1]
    chosen = route_row_ref[...]
    kinds = lax.broadcasted_iota(jnp.int32, (experts, count), 0)
    onehot = (chosen == kinds).astype(jnp.bfloat16)
    earlier = (lax.broadcasted_iota(jnp.int32, (count, count), 0)
               < lax.broadcasted_iota(jnp.int32, (count, count), 1)).astype(jnp.bfloat16)
    before = jnp.dot(onehot, earlier, preferred_element_type=jnp.float32)
    ranks = jnp.sum(before * onehot.astype(jnp.float32), axis=0, keepdims=True).astype(jnp.int32)
    target = chosen * capacity + ranks
    slots = lax.broadcasted_iota(jnp.int32, (slot_count, count), 0)
    placer = (slots == target).astype(jnp.bfloat16)
    placer_ref[...] = placer
    gather_ref[...] = jnp.transpose(placer)
    loads[0].wait()
    send_ref[:, :model] = jnp.dot(placer, tokens_ref[...], preferred_element_type=jnp.float32).astype(jnp.bfloat16)
    square = jnp.broadcast_to(weight_row_ref[...], (count, count))
    column = jnp.transpose(square)[:, :1]
    column_ref[...] = column
    loads[1].wait()
    cotangent = (column * grad_ref[...].astype(jnp.float32)).astype(jnp.bfloat16)
    send_ref[:, model:] = jnp.dot(placer, cotangent, preferred_element_type=jnp.float32).astype(jnp.bfloat16)


def dispatch_rows(routes, route_weight, tokens, out_grad, experts, capacity):
    count, model = tokens.shape
    vmem = pl.BlockSpec(memory_space=pltpu.VMEM)
    hbm = pl.BlockSpec(memory_space=pl.ANY)
    return pl.pallas_call(
        functools.partial(dispatch_kernel, experts),
        out_shape=(
            jax.ShapeDtypeStruct((experts * capacity, 2 * model), jnp.bfloat16),
            jax.ShapeDtypeStruct((experts * capacity, count), jnp.bfloat16),
            jax.ShapeDtypeStruct((count, experts * capacity), jnp.bfloat16),
            jax.ShapeDtypeStruct((count, 1), jnp.float32),
        ),
        in_specs=[hbm, hbm, hbm, hbm],
        out_specs=(vmem, vmem, vmem, vmem),
        scratch_shapes=[
            pltpu.VMEM((1, count), jnp.int32),
            pltpu.VMEM((1, count), jnp.float32),
            pltpu.VMEM(tokens.shape, tokens.dtype),
            pltpu.VMEM(out_grad.shape, out_grad.dtype),
            pltpu.SemaphoreType.DMA((4,)),
        ],
        compiler_params=pltpu.CompilerParams(vmem_limit_bytes=16 * 1024 * 1024),
        cost_estimate=pl.CostEstimate(
            flops=2 * experts * capacity * count * 2 * model,
            bytes_accessed=2 * (2 * count * model + experts * capacity * 2 * model),
            transcendentals=0),
    )(
        pltpu.with_memory_space_constraint(routes.reshape(1, count), pltpu.HBM),
        pltpu.with_memory_space_constraint(route_weight.reshape(1, count), pltpu.HBM),
        pltpu.with_memory_space_constraint(tokens, pltpu.HBM),
        pltpu.with_memory_space_constraint(out_grad, pltpu.HBM),
    )


def combine_kernel(back_ref, gather_ref, weight_ref, mixed_ref, grad_ref):
    model = mixed_ref.shape[1]
    gather = gather_ref[...]
    mixed_ref[...] = (weight_ref[...] * jnp.dot(
        gather, back_ref[:, :model], preferred_element_type=jnp.float32)).astype(jnp.bfloat16)
    grad_ref[...] = jnp.dot(
        gather, back_ref[:, model:], preferred_element_type=jnp.float32).astype(jnp.bfloat16)


def combine_rows(back, gather, route_weight):
    count, slot_count = gather.shape
    model = back.shape[1] // 2
    vmem = pl.BlockSpec(memory_space=pltpu.VMEM)
    return pl.pallas_call(
        combine_kernel,
        out_shape=(
            jax.ShapeDtypeStruct((count, model), jnp.bfloat16),
            jax.ShapeDtypeStruct((count, model), jnp.bfloat16),
        ),
        in_specs=[vmem] * 3,
        out_specs=(vmem, vmem),
        compiler_params=pltpu.CompilerParams(vmem_limit_bytes=16 * 1024 * 1024),
        cost_estimate=pl.CostEstimate(
            flops=2 * count * slot_count * 2 * model,
            bytes_accessed=2 * (slot_count * 2 * model + 2 * count * model),
            transcendentals=0),
    )(pltpu.with_memory_space_constraint(back, pltpu.VMEM), gather, route_weight)


def per_device(tokens, routes, route_weight, w_in, w_out, out_grad):
    token_count, model = tokens.shape
    experts = w_in.shape[0] * lax.axis_size("expert")
    capacity = 3 * token_count // (2 * experts)
    width = w_out.shape[2]
    replicas = lax.axis_size("dp")
    first = w_in[0]
    second = w_out[0]
    send, placer, gather, column = dispatch_rows(routes, route_weight, tokens, out_grad, experts, capacity)
    recv = lax.all_to_all(send, "expert", split_axis=0, concat_axis=0, tiled=True)
    payload, hidden, grad_both = expert_rows(recv, first, second)
    rows_in = recv[:, :model]
    rows_cot = recv[:, model:]
    back = lax.all_to_all(payload, "expert", split_axis=0, concat_axis=0, tiled=True)
    mixed, token_grad = combine_rows(back, gather, column)
    halves = []
    for rows, right in ((rows_in, grad_both), (rows_cot, hidden)):
        ordered = halving_order(rows, "dp")
        middle = ordered.shape[1] // 2
        halves.append(tuple(
            contract_rows(piece, right).astype(jnp.bfloat16)
            for piece in (ordered[:, :middle], ordered[:, middle:])
        ))
    sum_first, sum_second = reduce_scatter_rows(halves, "dp")
    grad_in = (sum_first / replicas).astype(jnp.bfloat16)[None]
    grad_out = (sum_second / replicas).astype(jnp.bfloat16)[None]
    return (mixed, token_grad, grad_in, grad_out)


def solution(mesh):
    in_specs = (
        P(("expert", "dp"), None),
        P(("expert", "dp"), None),
        P(("expert", "dp"), None),
        P("expert", None, None),
        P("expert", None, None),
        P(("expert", "dp"), None),
    )
    out_specs = (
        P(("expert", "dp"), None),
        P(("expert", "dp"), None),
        P("expert", "dp", None),
        P("expert", "dp", None),
    )
    return jax.shard_map(
        per_device, mesh=mesh, in_specs=in_specs, out_specs=out_specs, check_vma=False
    )
```

```python
import functools

import jax
import jax.numpy as jnp
from jax import lax
from jax.experimental import pallas as pl
from jax.experimental.pallas import tpu as pltpu
from jax.sharding import PartitionSpec as P


def contract_rows(left, right):
    return lax.dot_general(
        left, right, (((0,), (0,)), ((), ())), preferred_element_type=jnp.float32
    )


def contract_cols(left, right):
    return lax.dot_general(
        left, right, (((1,), (1,)), ((), ())), preferred_element_type=jnp.float32
    )


def halving_order(rows, axis):
    size = lax.axis_size(axis)
    me = lax.axis_index(axis)
    bits = size.bit_length() - 1
    share = rows.shape[1] // size
    parts = []
    for p in range(size):
        rev = int(format(p, "0{}b".format(bits))[::-1], 2) if bits else 0
        start = (me ^ rev) * share
        parts.append(lax.dynamic_slice_in_dim(rows, start, share, axis=1))
    return jnp.concatenate(parts, axis=1)


def reduce_scatter_rows(halves, axis):
    size = lax.axis_size(axis)
    step = 1
    kept = [k.astype(jnp.float32) for k, _ in halves]
    sent = [t for _, t in halves]
    while True:
        perm = [(k, k ^ step) for k in range(size)]
        got = [lax.ppermute(t.astype(jnp.bfloat16), axis, perm) for t in sent]
        total = [k + g.astype(jnp.float32) for k, g in zip(kept, got)]
        step *= 2
        if step >= size:
            return total
        half = total[0].shape[0] // 2
        kept = [t[:half] for t in total]
        sent = [t[half:] for t in total]


def expert_kernel(inline, me_ref, recv_ref, w_in_hbm, w_out_hbm, pay_ref, hid_ref, q_ref,
                  *rest):
    x_ref, c_ref, w_in_ref, w_out_ref, sems = rest if inline else (None, None) + rest
    model = w_in_ref.shape[0]
    width = w_out_ref.shape[1]
    chunks = sems.shape[0] - 1
    depth = model // chunks
    loads = [
        pltpu.make_async_copy(
            w_in_hbm.at[pl.ds(c * depth, depth)], w_in_ref.at[pl.ds(c * depth, depth)], sems.at[c])
        for c in range(chunks)
    ]
    w_out_load = pltpu.make_async_copy(w_out_hbm, w_out_ref, sems.at[chunks])
    for load in loads:
        load.start()
    w_out_load.start()
    gate_up = None
    for c, load in enumerate(loads):
        load.wait()
        band = pl.ds(c * depth, depth)
        part = jnp.dot(recv_ref[:, band], w_in_ref[band, :], preferred_element_type=jnp.float32)
        gate_up = part if gate_up is None else gate_up + part
    size = me_ref.shape[0]
    share = model // size
    bits = size.bit_length() - 1
    me = me_ref[0]
    for p in range(size if inline else 0):
        rev = int(format(p, "0{}b".format(bits))[::-1], 2) if bits else 0
        start = pl.multiple_of((me ^ rev) * share, share)
        x_ref[:, p * share:(p + 1) * share] = recv_ref[:, pl.ds(start, share)]
        c_ref[:, p * share:(p + 1) * share] = recv_ref[:, pl.ds(start + model, share)]
    w_out_load.wait()
    w_in = w_in_ref[...]
    w_out = w_out_ref[...]
    gate = gate_up[:, :width]
    upper = gate_up[:, width:]
    sigmoid_gate = 1.0 / (1.0 + jnp.exp(-gate))
    activated = gate * sigmoid_gate
    hidden = (activated * upper).astype(jnp.bfloat16)
    hid_ref[...] = hidden
    pay_ref[:, :model] = contract_cols(hidden, w_out).astype(jnp.bfloat16)
    grad_hidden = jnp.dot(recv_ref[:, model:], w_out, preferred_element_type=jnp.float32)
    grad_gate = grad_hidden * upper * sigmoid_gate * (1.0 + gate * (1.0 - sigmoid_gate))
    q_ref[:, :width] = grad_gate.astype(jnp.bfloat16)
    q_ref[:, width:] = (grad_hidden * activated).astype(jnp.bfloat16)
    pay_ref[:, model:] = contract_cols(q_ref[...], w_in).astype(jnp.bfloat16)


def expert_rows(recv, first, second):
    rows = recv.shape[0]
    model, width = second.shape
    chunks = 4 if model % 64 == 0 else 1
    vmem = pl.BlockSpec(memory_space=pltpu.VMEM)
    hbm = pl.BlockSpec(memory_space=pl.ANY)
    flops = 2 * rows * model * width * 6
    moved = 2 * (2 * rows * 2 * model + model * 3 * width + rows * 3 * width)
    inline = (model // lax.axis_size("dp")) % 128 == 0
    outs = pl.pallas_call(
        functools.partial(expert_kernel, inline),
        out_shape=(
            jax.ShapeDtypeStruct((rows, 2 * model), jnp.bfloat16),
            jax.ShapeDtypeStruct((rows, width), jnp.bfloat16),
            jax.ShapeDtypeStruct((rows, 2 * width), jnp.bfloat16),
        ) + (jax.ShapeDtypeStruct((rows, model), jnp.bfloat16),) * (2 if inline else 0),
        in_specs=[pl.BlockSpec(memory_space=pltpu.SMEM), vmem, hbm, hbm],
        out_specs=(vmem,) * (5 if inline else 3),
        scratch_shapes=[
            pltpu.VMEM(first.shape, first.dtype),
            pltpu.VMEM(second.shape, second.dtype),
            pltpu.SemaphoreType.DMA((chunks + 1,)),
        ],
        compiler_params=pltpu.CompilerParams(vmem_limit_bytes=24 * 1024 * 1024),
        cost_estimate=pl.CostEstimate(
            flops=flops, bytes_accessed=moved, transcendentals=rows * width),
    )(
        jnp.full((lax.axis_size("dp"),), lax.axis_index("dp"), jnp.int32),
        pltpu.with_memory_space_constraint(recv, pltpu.VMEM),
        pltpu.with_memory_space_constraint(first, pltpu.HBM),
        pltpu.with_memory_space_constraint(second, pltpu.HBM),
    )
    if inline:
        return outs
    return outs + (halving_order(recv[:, :model], "dp"), halving_order(recv[:, model:], "dp"))


def dispatch_kernel(experts, route_hbm, weight_hbm, tokens_hbm, grad_hbm, send_ref,
                    placer_ref, gather_ref, column_ref, route_row_ref, weight_row_ref,
                    tokens_ref, grad_ref, sems):
    rows_in = [
        pltpu.make_async_copy(route_hbm, route_row_ref, sems.at[2]),
        pltpu.make_async_copy(weight_hbm, weight_row_ref, sems.at[3]),
    ]
    loads = [
        pltpu.make_async_copy(tokens_hbm, tokens_ref, sems.at[0]),
        pltpu.make_async_copy(grad_hbm, grad_ref, sems.at[1]),
    ]
    for load in rows_in + loads:
        load.start()
    for load in rows_in:
        load.wait()
    slot_count, count = send_ref.shape[0], route_row_ref.shape[1]
    capacity = slot_count // experts
    model = tokens_ref.shape[1]
    chosen = route_row_ref[...]
    kinds = lax.broadcasted_iota(jnp.int32, (experts, count), 0)
    onehot = (chosen == kinds).astype(jnp.bfloat16)
    earlier = (lax.broadcasted_iota(jnp.int32, (count, count), 0)
               < lax.broadcasted_iota(jnp.int32, (count, count), 1)).astype(jnp.bfloat16)
    before = jnp.dot(onehot, earlier, preferred_element_type=jnp.float32)
    ranks = jnp.sum(before * onehot.astype(jnp.float32), axis=0, keepdims=True).astype(jnp.int32)
    target = chosen * capacity + ranks
    slots = lax.broadcasted_iota(jnp.int32, (slot_count, count), 0)
    placer = (slots == target).astype(jnp.bfloat16)
    placer_ref[...] = placer
    gather_ref[...] = jnp.transpose(placer)
    loads[0].wait()
    send_ref[:, :model] = jnp.dot(placer, tokens_ref[...], preferred_element_type=jnp.float32).astype(jnp.bfloat16)
    square = jnp.broadcast_to(weight_row_ref[...], (count, count))
    column = jnp.transpose(square)[:, :1]
    column_ref[...] = column
    loads[1].wait()
    cotangent = (column * grad_ref[...].astype(jnp.float32)).astype(jnp.bfloat16)
    send_ref[:, model:] = jnp.dot(placer, cotangent, preferred_element_type=jnp.float32).astype(jnp.bfloat16)


def dispatch_rows(routes, route_weight, tokens, out_grad, experts, capacity):
    count, model = tokens.shape
    vmem = pl.BlockSpec(memory_space=pltpu.VMEM)
    hbm = pl.BlockSpec(memory_space=pl.ANY)
    return pl.pallas_call(
        functools.partial(dispatch_kernel, experts),
        out_shape=(
            jax.ShapeDtypeStruct((experts * capacity, 2 * model), jnp.bfloat16),
            jax.ShapeDtypeStruct((experts * capacity, count), jnp.bfloat16),
            jax.ShapeDtypeStruct((count, experts * capacity), jnp.bfloat16),
            jax.ShapeDtypeStruct((count, 1), jnp.float32),
        ),
        in_specs=[hbm, hbm, hbm, hbm],
        out_specs=(vmem, vmem, vmem, vmem),
        scratch_shapes=[
            pltpu.VMEM((1, count), jnp.int32),
            pltpu.VMEM((1, count), jnp.float32),
            pltpu.VMEM(tokens.shape, tokens.dtype),
            pltpu.VMEM(out_grad.shape, out_grad.dtype),
            pltpu.SemaphoreType.DMA((4,)),
        ],
        compiler_params=pltpu.CompilerParams(vmem_limit_bytes=16 * 1024 * 1024),
        cost_estimate=pl.CostEstimate(
            flops=2 * experts * capacity * count * 2 * model,
            bytes_accessed=2 * (2 * count * model + experts * capacity * 2 * model),
            transcendentals=0),
    )(
        pltpu.with_memory_space_constraint(routes.reshape(1, count), pltpu.HBM),
        pltpu.with_memory_space_constraint(route_weight.reshape(1, count), pltpu.HBM),
        pltpu.with_memory_space_constraint(tokens, pltpu.HBM),
        pltpu.with_memory_space_constraint(out_grad, pltpu.HBM),
    )


def combine_kernel(back_ref, gather_ref, weight_ref, mixed_ref, grad_ref):
    model = mixed_ref.shape[1]
    gather = gather_ref[...]
    mixed_ref[...] = (weight_ref[...] * jnp.dot(
        gather, back_ref[:, :model], preferred_element_type=jnp.float32)).astype(jnp.bfloat16)
    grad_ref[...] = jnp.dot(
        gather, back_ref[:, model:], preferred_element_type=jnp.float32).astype(jnp.bfloat16)


def combine_rows(back, gather, route_weight):
    count, slot_count = gather.shape
    model = back.shape[1] // 2
    vmem = pl.BlockSpec(memory_space=pltpu.VMEM)
    return pl.pallas_call(
        combine_kernel,
        out_shape=(
            jax.ShapeDtypeStruct((count, model), jnp.bfloat16),
            jax.ShapeDtypeStruct((count, model), jnp.bfloat16),
        ),
        in_specs=[vmem] * 3,
        out_specs=(vmem, vmem),
        compiler_params=pltpu.CompilerParams(vmem_limit_bytes=16 * 1024 * 1024),
        cost_estimate=pl.CostEstimate(
            flops=2 * count * slot_count * 2 * model,
            bytes_accessed=2 * (slot_count * 2 * model + 2 * count * model),
            transcendentals=0),
    )(pltpu.with_memory_space_constraint(back, pltpu.VMEM), gather, route_weight)


def per_device(tokens, routes, route_weight, w_in, w_out, out_grad):
    token_count, model = tokens.shape
    experts = w_in.shape[0] * lax.axis_size("expert")
    capacity = 3 * token_count // (2 * experts)
    width = w_out.shape[2]
    replicas = lax.axis_size("dp")
    first = w_in[0]
    second = w_out[0]
    send, placer, gather, column = dispatch_rows(routes, route_weight, tokens, out_grad, experts, capacity)
    recv = lax.all_to_all(send, "expert", split_axis=0, concat_axis=0, tiled=True)
    payload, hidden, grad_both, ordered_in, ordered_cot = expert_rows(recv, first, second)
    back = lax.all_to_all(payload, "expert", split_axis=0, concat_axis=0, tiled=True)
    mixed, token_grad = combine_rows(back, gather, column)
    halves = []
    for ordered, right in ((ordered_in, grad_both), (ordered_cot, hidden)):
        middle = ordered.shape[1] // 2
        halves.append(tuple(
            contract_rows(piece, right).astype(jnp.bfloat16)
            for piece in (ordered[:, :middle], ordered[:, middle:])
        ))
    sum_first, sum_second = reduce_scatter_rows(halves, "dp")
    grad_in = (sum_first / replicas).astype(jnp.bfloat16)[None]
    grad_out = (sum_second / replicas).astype(jnp.bfloat16)[None]
    return (mixed, token_grad, grad_in, grad_out)


def solution(mesh):
    in_specs = (
        P(("expert", "dp"), None),
        P(("expert", "dp"), None),
        P(("expert", "dp"), None),
        P("expert", None, None),
        P("expert", None, None),
        P(("expert", "dp"), None),
    )
    out_specs = (
        P(("expert", "dp"), None),
        P(("expert", "dp"), None),
        P("expert", "dp", None),
        P("expert", "dp", None),
    )
    return jax.shard_map(
        per_device, mesh=mesh, in_specs=in_specs, out_specs=out_specs, check_vma=False
    )
```

```python
import functools

import jax
import jax.numpy as jnp
from jax import lax
from jax.experimental import pallas as pl
from jax.experimental.pallas import tpu as pltpu
from jax.sharding import PartitionSpec as P


def contract_rows(left, right):
    return lax.dot_general(
        left, right, (((0,), (0,)), ((), ())), preferred_element_type=jnp.float32
    )


def contract_cols(left, right):
    return lax.dot_general(
        left, right, (((1,), (1,)), ((), ())), preferred_element_type=jnp.float32
    )


def halving_order(rows, axis):
    size = lax.axis_size(axis)
    me = lax.axis_index(axis)
    bits = size.bit_length() - 1
    share = rows.shape[1] // size
    parts = []
    for p in range(size):
        rev = int(format(p, "0{}b".format(bits))[::-1], 2) if bits else 0
        start = (me ^ rev) * share
        parts.append(lax.dynamic_slice_in_dim(rows, start, share, axis=1))
    return jnp.concatenate(parts, axis=1)


def reduce_scatter_rows(halves, axis):
    size = lax.axis_size(axis)
    step = 1
    kept = [k.astype(jnp.float32) for k, _ in halves]
    sent = [t for _, t in halves]
    while True:
        perm = [(k, k ^ step) for k in range(size)]
        got = [lax.ppermute(t.astype(jnp.bfloat16), axis, perm) for t in sent]
        total = [k + g.astype(jnp.float32) for k, g in zip(kept, got)]
        step *= 2
        if step >= size:
            return total
        half = total[0].shape[0] // 2
        kept = [t[:half] for t in total]
        sent = [t[half:] for t in total]


def expert_kernel(recv_ref, w_in_hbm, w_out_hbm, pay_ref, hid_ref, q_ref,
                  w_in_ref, w_out_ref, sems):
    model = w_in_ref.shape[0]
    width = w_out_ref.shape[1]
    chunks = sems.shape[0] - 1
    depth = model // chunks
    loads = [
        pltpu.make_async_copy(
            w_in_hbm.at[pl.ds(c * depth, depth)], w_in_ref.at[pl.ds(c * depth, depth)], sems.at[c])
        for c in range(chunks)
    ]
    w_out_load = pltpu.make_async_copy(w_out_hbm, w_out_ref, sems.at[chunks])
    for load in loads:
        load.start()
    w_out_load.start()
    gate_up = None
    for c, load in enumerate(loads):
        load.wait()
        band = pl.ds(c * depth, depth)
        part = jnp.dot(recv_ref[:, band], w_in_ref[band, :], preferred_element_type=jnp.float32)
        gate_up = part if gate_up is None else gate_up + part
    w_out_load.wait()
    w_in = w_in_ref[...]
    w_out = w_out_ref[...]
    gate = gate_up[:, :width]
    upper = gate_up[:, width:]
    sigmoid_gate = 1.0 / (1.0 + jnp.exp(-gate))
    activated = gate * sigmoid_gate
    hidden = (activated * upper).astype(jnp.bfloat16)
    hid_ref[...] = hidden
    pay_ref[:, :model] = contract_cols(hidden, w_out).astype(jnp.bfloat16)
    grad_hidden = jnp.dot(recv_ref[:, model:], w_out, preferred_element_type=jnp.float32)
    grad_gate = grad_hidden * upper * sigmoid_gate * (1.0 + gate * (1.0 - sigmoid_gate))
    q_ref[:, :width] = grad_gate.astype(jnp.bfloat16)
    q_ref[:, width:] = (grad_hidden * activated).astype(jnp.bfloat16)
    pay_ref[:, model:] = contract_cols(q_ref[...], w_in).astype(jnp.bfloat16)


def expert_rows(recv, first, second):
    rows = recv.shape[0]
    model, width = second.shape
    chunks = 8 if model % 128 == 0 else 1
    vmem = pl.BlockSpec(memory_space=pltpu.VMEM)
    hbm = pl.BlockSpec(memory_space=pl.ANY)
    flops = 2 * rows * model * width * 6
    moved = 2 * (2 * rows * 2 * model + model * 3 * width + rows * 3 * width)
    return pl.pallas_call(
        expert_kernel,
        out_shape=(
            jax.ShapeDtypeStruct((rows, 2 * model), jnp.bfloat16),
            jax.ShapeDtypeStruct((rows, width), jnp.bfloat16),
            jax.ShapeDtypeStruct((rows, 2 * width), jnp.bfloat16),
        ),
        in_specs=[vmem, hbm, hbm],
        out_specs=(vmem, vmem, vmem),
        scratch_shapes=[
            pltpu.VMEM(first.shape, first.dtype),
            pltpu.VMEM(second.shape, second.dtype),
            pltpu.SemaphoreType.DMA((chunks + 1,)),
        ],
        compiler_params=pltpu.CompilerParams(vmem_limit_bytes=24 * 1024 * 1024),
        cost_estimate=pl.CostEstimate(
            flops=flops, bytes_accessed=moved, transcendentals=rows * width),
    )(
        pltpu.with_memory_space_constraint(recv, pltpu.VMEM),
        pltpu.with_memory_space_constraint(first, pltpu.HBM),
        pltpu.with_memory_space_constraint(second, pltpu.HBM),
    )


def dispatch_kernel(experts, route_hbm, weight_hbm, tokens_hbm, grad_hbm, send_ref,
                    placer_ref, gather_ref, column_ref, route_row_ref, weight_row_ref,
                    tokens_ref, grad_ref, sems):
    rows_in = [
        pltpu.make_async_copy(route_hbm, route_row_ref, sems.at[2]),
        pltpu.make_async_copy(weight_hbm, weight_row_ref, sems.at[3]),
    ]
    loads = [
        pltpu.make_async_copy(tokens_hbm, tokens_ref, sems.at[0]),
        pltpu.make_async_copy(grad_hbm, grad_ref, sems.at[1]),
    ]
    for load in rows_in + loads:
        load.start()
    for load in rows_in:
        load.wait()
    slot_count, count = send_ref.shape[0], route_row_ref.shape[1]
    capacity = slot_count // experts
    model = tokens_ref.shape[1]
    chosen = route_row_ref[...]
    kinds = lax.broadcasted_iota(jnp.int32, (experts, count), 0)
    onehot = (chosen == kinds).astype(jnp.bfloat16)
    earlier = (lax.broadcasted_iota(jnp.int32, (count, count), 0)
               < lax.broadcasted_iota(jnp.int32, (count, count), 1)).astype(jnp.bfloat16)
    before = jnp.dot(onehot, earlier, preferred_element_type=jnp.float32)
    ranks = jnp.sum(before * onehot.astype(jnp.float32), axis=0, keepdims=True).astype(jnp.int32)
    target = chosen * capacity + ranks
    slots = lax.broadcasted_iota(jnp.int32, (slot_count, count), 0)
    placer = (slots == target).astype(jnp.bfloat16)
    placer_ref[...] = placer
    gather_ref[...] = jnp.transpose(placer)
    loads[0].wait()
    send_ref[:, :model] = jnp.dot(placer, tokens_ref[...], preferred_element_type=jnp.float32).astype(jnp.bfloat16)
    square = jnp.broadcast_to(weight_row_ref[...], (count, count))
    column = jnp.transpose(square)[:, :1]
    column_ref[...] = column
    loads[1].wait()
    cotangent = (column * grad_ref[...].astype(jnp.float32)).astype(jnp.bfloat16)
    send_ref[:, model:] = jnp.dot(placer, cotangent, preferred_element_type=jnp.float32).astype(jnp.bfloat16)


def dispatch_rows(routes, route_weight, tokens, out_grad, experts, capacity):
    count, model = tokens.shape
    vmem = pl.BlockSpec(memory_space=pltpu.VMEM)
    hbm = pl.BlockSpec(memory_space=pl.ANY)
    return pl.pallas_call(
        functools.partial(dispatch_kernel, experts),
        out_shape=(
            jax.ShapeDtypeStruct((experts * capacity, 2 * model), jnp.bfloat16),
            jax.ShapeDtypeStruct((experts * capacity, count), jnp.bfloat16),
            jax.ShapeDtypeStruct((count, experts * capacity), jnp.bfloat16),
            jax.ShapeDtypeStruct((count, 1), jnp.float32),
        ),
        in_specs=[hbm, hbm, hbm, hbm],
        out_specs=(vmem, vmem, vmem, vmem),
        scratch_shapes=[
            pltpu.VMEM((1, count), jnp.int32),
            pltpu.VMEM((1, count), jnp.float32),
            pltpu.VMEM(tokens.shape, tokens.dtype),
            pltpu.VMEM(out_grad.shape, out_grad.dtype),
            pltpu.SemaphoreType.DMA((4,)),
        ],
        compiler_params=pltpu.CompilerParams(vmem_limit_bytes=16 * 1024 * 1024),
        cost_estimate=pl.CostEstimate(
            flops=2 * experts * capacity * count * 2 * model,
            bytes_accessed=2 * (2 * count * model + experts * capacity * 2 * model),
            transcendentals=0),
    )(
        pltpu.with_memory_space_constraint(routes.reshape(1, count), pltpu.HBM),
        pltpu.with_memory_space_constraint(route_weight.reshape(1, count), pltpu.HBM),
        pltpu.with_memory_space_constraint(tokens, pltpu.HBM),
        pltpu.with_memory_space_constraint(out_grad, pltpu.HBM),
    )


def combine_kernel(back_ref, gather_ref, weight_ref, mixed_ref, grad_ref):
    model = mixed_ref.shape[1]
    gather = gather_ref[...]
    mixed_ref[...] = (weight_ref[...] * jnp.dot(
        gather, back_ref[:, :model], preferred_element_type=jnp.float32)).astype(jnp.bfloat16)
    grad_ref[...] = jnp.dot(
        gather, back_ref[:, model:], preferred_element_type=jnp.float32).astype(jnp.bfloat16)


def combine_rows(back, gather, route_weight):
    count, slot_count = gather.shape
    model = back.shape[1] // 2
    vmem = pl.BlockSpec(memory_space=pltpu.VMEM)
    return pl.pallas_call(
        combine_kernel,
        out_shape=(
            jax.ShapeDtypeStruct((count, model), jnp.bfloat16),
            jax.ShapeDtypeStruct((count, model), jnp.bfloat16),
        ),
        in_specs=[vmem] * 3,
        out_specs=(vmem, vmem),
        compiler_params=pltpu.CompilerParams(vmem_limit_bytes=16 * 1024 * 1024),
        cost_estimate=pl.CostEstimate(
            flops=2 * count * slot_count * 2 * model,
            bytes_accessed=2 * (slot_count * 2 * model + 2 * count * model),
            transcendentals=0),
    )(pltpu.with_memory_space_constraint(back, pltpu.VMEM), gather, route_weight)


def per_device(tokens, routes, route_weight, w_in, w_out, out_grad):
    token_count, model = tokens.shape
    experts = w_in.shape[0] * lax.axis_size("expert")
    capacity = 3 * token_count // (2 * experts)
    width = w_out.shape[2]
    replicas = lax.axis_size("dp")
    first = w_in[0]
    second = w_out[0]
    send, placer, gather, column = dispatch_rows(routes, route_weight, tokens, out_grad, experts, capacity)
    recv = lax.all_to_all(send, "expert", split_axis=0, concat_axis=0, tiled=True)
    payload, hidden, grad_both = expert_rows(recv, first, second)
    rows_in = recv[:, :model]
    rows_cot = recv[:, model:]
    back = lax.all_to_all(payload, "expert", split_axis=0, concat_axis=0, tiled=True)
    mixed, token_grad = combine_rows(back, gather, column)
    halves = []
    for rows, right in ((rows_in, grad_both), (rows_cot, hidden)):
        ordered = halving_order(rows, "dp")
        middle = ordered.shape[1] // 2
        halves.append(tuple(
            contract_rows(piece, right).astype(jnp.bfloat16)
            for piece in (ordered[:, :middle], ordered[:, middle:])
        ))
    sum_first, sum_second = reduce_scatter_rows(halves, "dp")
    grad_in = (sum_first / replicas).astype(jnp.bfloat16)[None]
    grad_out = (sum_second / replicas).astype(jnp.bfloat16)[None]
    return (mixed, token_grad, grad_in, grad_out)


def solution(mesh):
    in_specs = (
        P(("expert", "dp"), None),
        P(("expert", "dp"), None),
        P(("expert", "dp"), None),
        P("expert", None, None),
        P("expert", None, None),
        P(("expert", "dp"), None),
    )
    out_specs = (
        P(("expert", "dp"), None),
        P(("expert", "dp"), None),
        P("expert", "dp", None),
        P("expert", "dp", None),
    )
    return jax.shard_map(
        per_device, mesh=mesh, in_specs=in_specs, out_specs=out_specs, check_vma=False
    )
```

```python
import functools

import jax
import jax.numpy as jnp
from jax import lax
from jax.experimental import pallas as pl
from jax.experimental.pallas import tpu as pltpu
from jax.sharding import PartitionSpec as P


def contract_rows(left, right):
    return lax.dot_general(
        left, right, (((0,), (0,)), ((), ())), preferred_element_type=jnp.float32
    )


def contract_cols(left, right):
    return lax.dot_general(
        left, right, (((1,), (1,)), ((), ())), preferred_element_type=jnp.float32
    )


def halving_order(rows, axis):
    size = lax.axis_size(axis)
    me = lax.axis_index(axis)
    bits = size.bit_length() - 1
    share = rows.shape[1] // size
    parts = []
    for p in range(size):
        rev = int(format(p, "0{}b".format(bits))[::-1], 2) if bits else 0
        start = (me ^ rev) * share
        parts.append(lax.dynamic_slice_in_dim(rows, start, share, axis=1))
    return jnp.concatenate(parts, axis=1)


def reduce_scatter_rows(halves, axis):
    size = lax.axis_size(axis)
    step = 1
    kept = [k.astype(jnp.float32) for k, _ in halves]
    sent = [t for _, t in halves]
    while True:
        perm = [(k, k ^ step) for k in range(size)]
        got = [lax.ppermute(t.astype(jnp.bfloat16), axis, perm) for t in sent]
        total = [k + g.astype(jnp.float32) for k, g in zip(kept, got)]
        step *= 2
        if step >= size:
            return total
        half = total[0].shape[0] // 2
        kept = [t[:half] for t in total]
        sent = [t[half:] for t in total]


def expert_kernel(recv_ref, w_in_hbm, w_out_hbm, pay_ref, hid_ref, q_ref,
                  w_in_ref, w_out_ref, sems):
    model = w_in_ref.shape[0]
    width = w_out_ref.shape[1]
    chunks = sems.shape[0] - 1
    depth = model // chunks
    loads = [
        pltpu.make_async_copy(
            w_in_hbm.at[pl.ds(c * depth, depth)], w_in_ref.at[pl.ds(c * depth, depth)], sems.at[c])
        for c in range(chunks)
    ]
    w_out_load = pltpu.make_async_copy(w_out_hbm, w_out_ref, sems.at[chunks])
    for load in loads:
        load.start()
    w_out_load.start()
    gate_up = None
    for c, load in enumerate(loads):
        load.wait()
        band = pl.ds(c * depth, depth)
        part = jnp.dot(recv_ref[:, band], w_in_ref[band, :], preferred_element_type=jnp.float32)
        gate_up = part if gate_up is None else gate_up + part
    w_out_load.wait()
    w_in = w_in_ref[...]
    w_out = w_out_ref[...]
    gate = gate_up[:, :width]
    upper = gate_up[:, width:]
    sigmoid_gate = 1.0 / (1.0 + jnp.exp(-gate))
    activated = gate * sigmoid_gate
    hidden = (activated * upper).astype(jnp.bfloat16)
    hid_ref[...] = hidden
    pay_ref[:, :model] = contract_cols(hidden, w_out).astype(jnp.bfloat16)
    grad_hidden = jnp.dot(recv_ref[:, model:], w_out, preferred_element_type=jnp.float32)
    grad_gate = grad_hidden * upper * sigmoid_gate * (1.0 + gate * (1.0 - sigmoid_gate))
    q_ref[:, :width] = grad_gate.astype(jnp.bfloat16)
    q_ref[:, width:] = (grad_hidden * activated).astype(jnp.bfloat16)
    pay_ref[:, model:] = contract_cols(q_ref[...], w_in).astype(jnp.bfloat16)


def expert_rows(recv, first, second):
    rows = recv.shape[0]
    model, width = second.shape
    chunks = 16 if model % 256 == 0 else 1
    vmem = pl.BlockSpec(memory_space=pltpu.VMEM)
    hbm = pl.BlockSpec(memory_space=pl.ANY)
    flops = 2 * rows * model * width * 6
    moved = 2 * (2 * rows * 2 * model + model * 3 * width + rows * 3 * width)
    return pl.pallas_call(
        expert_kernel,
        out_shape=(
            jax.ShapeDtypeStruct((rows, 2 * model), jnp.bfloat16),
            jax.ShapeDtypeStruct((rows, width), jnp.bfloat16),
            jax.ShapeDtypeStruct((rows, 2 * width), jnp.bfloat16),
        ),
        in_specs=[vmem, hbm, hbm],
        out_specs=(vmem, vmem, vmem),
        scratch_shapes=[
            pltpu.VMEM(first.shape, first.dtype),
            pltpu.VMEM(second.shape, second.dtype),
            pltpu.SemaphoreType.DMA((chunks + 1,)),
        ],
        compiler_params=pltpu.CompilerParams(vmem_limit_bytes=24 * 1024 * 1024),
        cost_estimate=pl.CostEstimate(
            flops=flops, bytes_accessed=moved, transcendentals=rows * width),
    )(
        pltpu.with_memory_space_constraint(recv, pltpu.VMEM),
        pltpu.with_memory_space_constraint(first, pltpu.HBM),
        pltpu.with_memory_space_constraint(second, pltpu.HBM),
    )


def dispatch_kernel(experts, route_hbm, weight_hbm, tokens_hbm, grad_hbm, send_ref,
                    placer_ref, gather_ref, column_ref, route_row_ref, weight_row_ref,
                    tokens_ref, grad_ref, sems):
    rows_in = [
        pltpu.make_async_copy(route_hbm, route_row_ref, sems.at[2]),
        pltpu.make_async_copy(weight_hbm, weight_row_ref, sems.at[3]),
    ]
    loads = [
        pltpu.make_async_copy(tokens_hbm, tokens_ref, sems.at[0]),
        pltpu.make_async_copy(grad_hbm, grad_ref, sems.at[1]),
    ]
    for load in rows_in + loads:
        load.start()
    for load in rows_in:
        load.wait()
    slot_count, count = send_ref.shape[0], route_row_ref.shape[1]
    capacity = slot_count // experts
    model = tokens_ref.shape[1]
    chosen = route_row_ref[...]
    kinds = lax.broadcasted_iota(jnp.int32, (experts, count), 0)
    onehot = (chosen == kinds).astype(jnp.bfloat16)
    earlier = (lax.broadcasted_iota(jnp.int32, (count, count), 0)
               < lax.broadcasted_iota(jnp.int32, (count, count), 1)).astype(jnp.bfloat16)
    before = jnp.dot(onehot, earlier, preferred_element_type=jnp.float32)
    ranks = jnp.sum(before * onehot.astype(jnp.float32), axis=0, keepdims=True).astype(jnp.int32)
    target = chosen * capacity + ranks
    slots = lax.broadcasted_iota(jnp.int32, (slot_count, count), 0)
    placer = (slots == target).astype(jnp.bfloat16)
    placer_ref[...] = placer
    gather_ref[...] = jnp.transpose(placer)
    loads[0].wait()
    send_ref[:, :model] = jnp.dot(placer, tokens_ref[...], preferred_element_type=jnp.float32).astype(jnp.bfloat16)
    square = jnp.broadcast_to(weight_row_ref[...], (count, count))
    column = jnp.transpose(square)[:, :1]
    column_ref[...] = column
    loads[1].wait()
    cotangent = (column * grad_ref[...].astype(jnp.float32)).astype(jnp.bfloat16)
    send_ref[:, model:] = jnp.dot(placer, cotangent, preferred_element_type=jnp.float32).astype(jnp.bfloat16)


def dispatch_rows(routes, route_weight, tokens, out_grad, experts, capacity):
    count, model = tokens.shape
    vmem = pl.BlockSpec(memory_space=pltpu.VMEM)
    hbm = pl.BlockSpec(memory_space=pl.ANY)
    return pl.pallas_call(
        functools.partial(dispatch_kernel, experts),
        out_shape=(
            jax.ShapeDtypeStruct((experts * capacity, 2 * model), jnp.bfloat16),
            jax.ShapeDtypeStruct((experts * capacity, count), jnp.bfloat16),
            jax.ShapeDtypeStruct((count, experts * capacity), jnp.bfloat16),
            jax.ShapeDtypeStruct((count, 1), jnp.float32),
        ),
        in_specs=[hbm, hbm, hbm, hbm],
        out_specs=(vmem, vmem, vmem, vmem),
        scratch_shapes=[
            pltpu.VMEM((1, count), jnp.int32),
            pltpu.VMEM((1, count), jnp.float32),
            pltpu.VMEM(tokens.shape, tokens.dtype),
            pltpu.VMEM(out_grad.shape, out_grad.dtype),
            pltpu.SemaphoreType.DMA((4,)),
        ],
        compiler_params=pltpu.CompilerParams(vmem_limit_bytes=16 * 1024 * 1024),
        cost_estimate=pl.CostEstimate(
            flops=2 * experts * capacity * count * 2 * model,
            bytes_accessed=2 * (2 * count * model + experts * capacity * 2 * model),
            transcendentals=0),
    )(
        pltpu.with_memory_space_constraint(routes.reshape(1, count), pltpu.HBM),
        pltpu.with_memory_space_constraint(route_weight.reshape(1, count), pltpu.HBM),
        pltpu.with_memory_space_constraint(tokens, pltpu.HBM),
        pltpu.with_memory_space_constraint(out_grad, pltpu.HBM),
    )


def combine_kernel(back_ref, gather_ref, weight_ref, mixed_ref, grad_ref):
    model = mixed_ref.shape[1]
    gather = gather_ref[...]
    mixed_ref[...] = (weight_ref[...] * jnp.dot(
        gather, back_ref[:, :model], preferred_element_type=jnp.float32)).astype(jnp.bfloat16)
    grad_ref[...] = jnp.dot(
        gather, back_ref[:, model:], preferred_element_type=jnp.float32).astype(jnp.bfloat16)


def combine_rows(back, gather, route_weight):
    count, slot_count = gather.shape
    model = back.shape[1] // 2
    vmem = pl.BlockSpec(memory_space=pltpu.VMEM)
    return pl.pallas_call(
        combine_kernel,
        out_shape=(
            jax.ShapeDtypeStruct((count, model), jnp.bfloat16),
            jax.ShapeDtypeStruct((count, model), jnp.bfloat16),
        ),
        in_specs=[vmem] * 3,
        out_specs=(vmem, vmem),
        compiler_params=pltpu.CompilerParams(vmem_limit_bytes=16 * 1024 * 1024),
        cost_estimate=pl.CostEstimate(
            flops=2 * count * slot_count * 2 * model,
            bytes_accessed=2 * (slot_count * 2 * model + 2 * count * model),
            transcendentals=0),
    )(pltpu.with_memory_space_constraint(back, pltpu.VMEM), gather, route_weight)


def per_device(tokens, routes, route_weight, w_in, w_out, out_grad):
    token_count, model = tokens.shape
    experts = w_in.shape[0] * lax.axis_size("expert")
    capacity = 3 * token_count // (2 * experts)
    width = w_out.shape[2]
    replicas = lax.axis_size("dp")
    first = w_in[0]
    second = w_out[0]
    send, placer, gather, column = dispatch_rows(routes, route_weight, tokens, out_grad, experts, capacity)
    recv = lax.all_to_all(send, "expert", split_axis=0, concat_axis=0, tiled=True)
    payload, hidden, grad_both = expert_rows(recv, first, second)
    rows_in = recv[:, :model]
    rows_cot = recv[:, model:]
    back = lax.all_to_all(payload, "expert", split_axis=0, concat_axis=0, tiled=True)
    mixed, token_grad = combine_rows(back, gather, column)
    halves = []
    for rows, right in ((rows_in, grad_both), (rows_cot, hidden)):
        ordered = halving_order(rows, "dp")
        middle = ordered.shape[1] // 2
        halves.append(tuple(
            contract_rows(piece, right).astype(jnp.bfloat16)
            for piece in (ordered[:, :middle], ordered[:, middle:])
        ))
    sum_first, sum_second = reduce_scatter_rows(halves, "dp")
    grad_in = (sum_first / replicas).astype(jnp.bfloat16)[None]
    grad_out = (sum_second / replicas).astype(jnp.bfloat16)[None]
    return (mixed, token_grad, grad_in, grad_out)


def solution(mesh):
    in_specs = (
        P(("expert", "dp"), None),
        P(("expert", "dp"), None),
        P(("expert", "dp"), None),
        P("expert", None, None),
        P("expert", None, None),
        P(("expert", "dp"), None),
    )
    out_specs = (
        P(("expert", "dp"), None),
        P(("expert", "dp"), None),
        P("expert", "dp", None),
        P("expert", "dp", None),
    )
    return jax.shard_map(
        per_device, mesh=mesh, in_specs=in_specs, out_specs=out_specs, check_vma=False
    )
```

```python
import functools

import jax
import jax.numpy as jnp
from jax import lax
from jax.experimental import pallas as pl
from jax.experimental.pallas import tpu as pltpu
from jax.sharding import PartitionSpec as P


def contract_rows(left, right):
    return lax.dot_general(
        left, right, (((0,), (0,)), ((), ())), preferred_element_type=jnp.float32
    )


def contract_cols(left, right):
    return lax.dot_general(
        left, right, (((1,), (1,)), ((), ())), preferred_element_type=jnp.float32
    )


def halving_order(rows, axis):
    size = lax.axis_size(axis)
    me = lax.axis_index(axis)
    bits = size.bit_length() - 1
    share = rows.shape[1] // size
    parts = []
    for p in range(size):
        rev = int(format(p, "0{}b".format(bits))[::-1], 2) if bits else 0
        start = (me ^ rev) * share
        parts.append(lax.dynamic_slice_in_dim(rows, start, share, axis=1))
    return jnp.concatenate(parts, axis=1)


def reduce_scatter_rows(halves, axis):
    size = lax.axis_size(axis)
    step = 1
    kept = [k.astype(jnp.float32) for k, _ in halves]
    sent = [t for _, t in halves]
    while True:
        perm = [(k, k ^ step) for k in range(size)]
        got = [lax.ppermute(t.astype(jnp.bfloat16), axis, perm) for t in sent]
        total = [k + g.astype(jnp.float32) for k, g in zip(kept, got)]
        step *= 2
        if step >= size:
            return total
        half = total[0].shape[0] // 2
        kept = [t[:half] for t in total]
        sent = [t[half:] for t in total]


def expert_kernel(recv_ref, w_in_hbm, w_out_hbm, pay_ref, hid_ref, q_ref,
                  w_in_ref, w_out_ref, sems):
    model = w_in_ref.shape[0]
    width = w_out_ref.shape[1]
    chunks = sems.shape[0] // 2
    depth = model // chunks
    loads = [
        pltpu.make_async_copy(
            w_in_hbm.at[pl.ds(c * depth, depth)], w_in_ref.at[pl.ds(c * depth, depth)], sems.at[c])
        for c in range(chunks)
    ]
    out_loads = [
        pltpu.make_async_copy(
            w_out_hbm.at[pl.ds(c * depth, depth)], w_out_ref.at[pl.ds(c * depth, depth)],
            sems.at[chunks + c])
        for c in range(chunks)
    ]
    for load in loads + out_loads:
        load.start()
    gate_up = None
    for c, load in enumerate(loads):
        load.wait()
        band = pl.ds(c * depth, depth)
        part = jnp.dot(recv_ref[:, band], w_in_ref[band, :], preferred_element_type=jnp.float32)
        gate_up = part if gate_up is None else gate_up + part
    grad_hidden = None
    for c, load in enumerate(out_loads):
        load.wait()
        band = pl.ds(c * depth, depth)
        part = jnp.dot(recv_ref[:, pl.ds(model + c * depth, depth)], w_out_ref[band, :],
                       preferred_element_type=jnp.float32)
        grad_hidden = part if grad_hidden is None else grad_hidden + part
    w_in = w_in_ref[...]
    w_out = w_out_ref[...]
    gate = gate_up[:, :width]
    upper = gate_up[:, width:]
    sigmoid_gate = 1.0 / (1.0 + jnp.exp(-gate))
    activated = gate * sigmoid_gate
    hidden = (activated * upper).astype(jnp.bfloat16)
    hid_ref[...] = hidden
    pay_ref[:, :model] = contract_cols(hidden, w_out).astype(jnp.bfloat16)
    grad_gate = grad_hidden * upper * sigmoid_gate * (1.0 + gate * (1.0 - sigmoid_gate))
    q_ref[:, :width] = grad_gate.astype(jnp.bfloat16)
    q_ref[:, width:] = (grad_hidden * activated).astype(jnp.bfloat16)
    pay_ref[:, model:] = contract_cols(q_ref[...], w_in).astype(jnp.bfloat16)


def expert_rows(recv, first, second):
    rows = recv.shape[0]
    model, width = second.shape
    chunks = 8 if model % 128 == 0 else 1
    vmem = pl.BlockSpec(memory_space=pltpu.VMEM)
    hbm = pl.BlockSpec(memory_space=pl.ANY)
    flops = 2 * rows * model * width * 6
    moved = 2 * (2 * rows * 2 * model + model * 3 * width + rows * 3 * width)
    return pl.pallas_call(
        expert_kernel,
        out_shape=(
            jax.ShapeDtypeStruct((rows, 2 * model), jnp.bfloat16),
            jax.ShapeDtypeStruct((rows, width), jnp.bfloat16),
            jax.ShapeDtypeStruct((rows, 2 * width), jnp.bfloat16),
        ),
        in_specs=[vmem, hbm, hbm],
        out_specs=(vmem, vmem, vmem),
        scratch_shapes=[
            pltpu.VMEM(first.shape, first.dtype),
            pltpu.VMEM(second.shape, second.dtype),
            pltpu.SemaphoreType.DMA((2 * chunks,)),
        ],
        compiler_params=pltpu.CompilerParams(vmem_limit_bytes=24 * 1024 * 1024),
        cost_estimate=pl.CostEstimate(
            flops=flops, bytes_accessed=moved, transcendentals=rows * width),
    )(
        pltpu.with_memory_space_constraint(recv, pltpu.VMEM),
        pltpu.with_memory_space_constraint(first, pltpu.HBM),
        pltpu.with_memory_space_constraint(second, pltpu.HBM),
    )


def dispatch_kernel(experts, route_hbm, weight_hbm, tokens_hbm, grad_hbm, send_ref,
                    placer_ref, gather_ref, column_ref, route_row_ref, weight_row_ref,
                    tokens_ref, grad_ref, sems):
    rows_in = [
        pltpu.make_async_copy(route_hbm, route_row_ref, sems.at[2]),
        pltpu.make_async_copy(weight_hbm, weight_row_ref, sems.at[3]),
    ]
    loads = [
        pltpu.make_async_copy(tokens_hbm, tokens_ref, sems.at[0]),
        pltpu.make_async_copy(grad_hbm, grad_ref, sems.at[1]),
    ]
    for load in rows_in + loads:
        load.start()
    for load in rows_in:
        load.wait()
    slot_count, count = send_ref.shape[0], route_row_ref.shape[1]
    capacity = slot_count // experts
    model = tokens_ref.shape[1]
    chosen = route_row_ref[...]
    kinds = lax.broadcasted_iota(jnp.int32, (experts, count), 0)
    onehot = (chosen == kinds).astype(jnp.bfloat16)
    earlier = (lax.broadcasted_iota(jnp.int32, (count, count), 0)
               < lax.broadcasted_iota(jnp.int32, (count, count), 1)).astype(jnp.bfloat16)
    before = jnp.dot(onehot, earlier, preferred_element_type=jnp.float32)
    ranks = jnp.sum(before * onehot.astype(jnp.float32), axis=0, keepdims=True).astype(jnp.int32)
    target = chosen * capacity + ranks
    slots = lax.broadcasted_iota(jnp.int32, (slot_count, count), 0)
    placer = (slots == target).astype(jnp.bfloat16)
    placer_ref[...] = placer
    gather_ref[...] = jnp.transpose(placer)
    loads[0].wait()
    send_ref[:, :model] = jnp.dot(placer, tokens_ref[...], preferred_element_type=jnp.float32).astype(jnp.bfloat16)
    square = jnp.broadcast_to(weight_row_ref[...], (count, count))
    column = jnp.transpose(square)[:, :1]
    column_ref[...] = column
    loads[1].wait()
    cotangent = (column * grad_ref[...].astype(jnp.float32)).astype(jnp.bfloat16)
    send_ref[:, model:] = jnp.dot(placer, cotangent, preferred_element_type=jnp.float32).astype(jnp.bfloat16)


def dispatch_rows(routes, route_weight, tokens, out_grad, experts, capacity):
    count, model = tokens.shape
    vmem = pl.BlockSpec(memory_space=pltpu.VMEM)
    hbm = pl.BlockSpec(memory_space=pl.ANY)
    return pl.pallas_call(
        functools.partial(dispatch_kernel, experts),
        out_shape=(
            jax.ShapeDtypeStruct((experts * capacity, 2 * model), jnp.bfloat16),
            jax.ShapeDtypeStruct((experts * capacity, count), jnp.bfloat16),
            jax.ShapeDtypeStruct((count, experts * capacity), jnp.bfloat16),
            jax.ShapeDtypeStruct((count, 1), jnp.float32),
        ),
        in_specs=[hbm, hbm, hbm, hbm],
        out_specs=(vmem, vmem, vmem, vmem),
        scratch_shapes=[
            pltpu.VMEM((1, count), jnp.int32),
            pltpu.VMEM((1, count), jnp.float32),
            pltpu.VMEM(tokens.shape, tokens.dtype),
            pltpu.VMEM(out_grad.shape, out_grad.dtype),
            pltpu.SemaphoreType.DMA((4,)),
        ],
        compiler_params=pltpu.CompilerParams(vmem_limit_bytes=16 * 1024 * 1024),
        cost_estimate=pl.CostEstimate(
            flops=2 * experts * capacity * count * 2 * model,
            bytes_accessed=2 * (2 * count * model + experts * capacity * 2 * model),
            transcendentals=0),
    )(
        pltpu.with_memory_space_constraint(routes.reshape(1, count), pltpu.HBM),
        pltpu.with_memory_space_constraint(route_weight.reshape(1, count), pltpu.HBM),
        pltpu.with_memory_space_constraint(tokens, pltpu.HBM),
        pltpu.with_memory_space_constraint(out_grad, pltpu.HBM),
    )


def combine_kernel(back_ref, gather_ref, weight_ref, mixed_ref, grad_ref):
    model = mixed_ref.shape[1]
    gather = gather_ref[...]
    mixed_ref[...] = (weight_ref[...] * jnp.dot(
        gather, back_ref[:, :model], preferred_element_type=jnp.float32)).astype(jnp.bfloat16)
    grad_ref[...] = jnp.dot(
        gather, back_ref[:, model:], preferred_element_type=jnp.float32).astype(jnp.bfloat16)


def combine_rows(back, gather, route_weight):
    count, slot_count = gather.shape
    model = back.shape[1] // 2
    vmem = pl.BlockSpec(memory_space=pltpu.VMEM)
    return pl.pallas_call(
        combine_kernel,
        out_shape=(
            jax.ShapeDtypeStruct((count, model), jnp.bfloat16),
            jax.ShapeDtypeStruct((count, model), jnp.bfloat16),
        ),
        in_specs=[vmem] * 3,
        out_specs=(vmem, vmem),
        compiler_params=pltpu.CompilerParams(vmem_limit_bytes=16 * 1024 * 1024),
        cost_estimate=pl.CostEstimate(
            flops=2 * count * slot_count * 2 * model,
            bytes_accessed=2 * (slot_count * 2 * model + 2 * count * model),
            transcendentals=0),
    )(pltpu.with_memory_space_constraint(back, pltpu.VMEM), gather, route_weight)


def per_device(tokens, routes, route_weight, w_in, w_out, out_grad):
    token_count, model = tokens.shape
    experts = w_in.shape[0] * lax.axis_size("expert")
    capacity = 3 * token_count // (2 * experts)
    width = w_out.shape[2]
    replicas = lax.axis_size("dp")
    first = w_in[0]
    second = w_out[0]
    send, placer, gather, column = dispatch_rows(routes, route_weight, tokens, out_grad, experts, capacity)
    recv = lax.all_to_all(send, "expert", split_axis=0, concat_axis=0, tiled=True)
    payload, hidden, grad_both = expert_rows(recv, first, second)
    rows_in = recv[:, :model]
    rows_cot = recv[:, model:]
    back = lax.all_to_all(payload, "expert", split_axis=0, concat_axis=0, tiled=True)
    mixed, token_grad = combine_rows(back, gather, column)
    halves = []
    for rows, right in ((rows_in, grad_both), (rows_cot, hidden)):
        ordered = halving_order(rows, "dp")
        middle = ordered.shape[1] // 2
        halves.append(tuple(
            contract_rows(piece, right).astype(jnp.bfloat16)
            for piece in (ordered[:, :middle], ordered[:, middle:])
        ))
    sum_first, sum_second = reduce_scatter_rows(halves, "dp")
    grad_in = (sum_first / replicas).astype(jnp.bfloat16)[None]
    grad_out = (sum_second / replicas).astype(jnp.bfloat16)[None]
    return (mixed, token_grad, grad_in, grad_out)


def solution(mesh):
    in_specs = (
        P(("expert", "dp"), None),
        P(("expert", "dp"), None),
        P(("expert", "dp"), None),
        P("expert", None, None),
        P("expert", None, None),
        P(("expert", "dp"), None),
    )
    out_specs = (
        P(("expert", "dp"), None),
        P(("expert", "dp"), None),
        P("expert", "dp", None),
        P("expert", "dp", None),
    )
    return jax.shard_map(
        per_device, mesh=mesh, in_specs=in_specs, out_specs=out_specs, check_vma=False
    )
```

```python
import functools

import jax
import jax.numpy as jnp
from jax import lax
from jax.experimental import pallas as pl
from jax.experimental.pallas import tpu as pltpu
from jax.sharding import PartitionSpec as P


def contract_rows(left, right):
    return lax.dot_general(
        left, right, (((0,), (0,)), ((), ())), preferred_element_type=jnp.float32
    )


def contract_cols(left, right):
    return lax.dot_general(
        left, right, (((1,), (1,)), ((), ())), preferred_element_type=jnp.float32
    )


def halving_order(rows, axis):
    size = lax.axis_size(axis)
    me = lax.axis_index(axis)
    bits = size.bit_length() - 1
    share = rows.shape[1] // size
    parts = []
    for p in range(size):
        rev = int(format(p, "0{}b".format(bits))[::-1], 2) if bits else 0
        start = (me ^ rev) * share
        parts.append(lax.dynamic_slice_in_dim(rows, start, share, axis=1))
    return jnp.concatenate(parts, axis=1)


def reduce_scatter_rows(halves, axis):
    size = lax.axis_size(axis)
    step = 1
    kept = [k.astype(jnp.float32) for k, _ in halves]
    sent = [t for _, t in halves]
    while True:
        perm = [(k, k ^ step) for k in range(size)]
        got = [lax.ppermute(t.astype(jnp.bfloat16), axis, perm) for t in sent]
        total = [k + g.astype(jnp.float32) for k, g in zip(kept, got)]
        step *= 2
        if step >= size:
            return total
        half = total[0].shape[0] // 2
        kept = [t[:half] for t in total]
        sent = [t[half:] for t in total]


def expert_kernel(recv_ref, w_in_hbm, w_out_hbm, pay_ref, hid_ref, q_ref,
                  w_in_ref, w_out_ref, sems):
    model = w_in_ref.shape[0]
    width = w_out_ref.shape[1]
    chunks = sems.shape[0] - 1
    depth = model // chunks
    loads = [
        pltpu.make_async_copy(
            w_in_hbm.at[pl.ds(c * depth, depth)], w_in_ref.at[pl.ds(c * depth, depth)], sems.at[c])
        for c in range(chunks)
    ]
    w_out_load = pltpu.make_async_copy(w_out_hbm, w_out_ref, sems.at[chunks])
    for load in loads:
        load.start()
    w_out_load.start()
    gate_up = None
    for c, load in enumerate(loads):
        load.wait()
        band = pl.ds(c * depth, depth)
        part = jnp.dot(recv_ref[:, band], w_in_ref[band, :], preferred_element_type=jnp.float32)
        gate_up = part if gate_up is None else gate_up + part
    w_out_load.wait()
    w_in = w_in_ref[...]
    w_out = w_out_ref[...]
    gate = gate_up[:, :width]
    upper = gate_up[:, width:]
    sigmoid_gate = 1.0 / (1.0 + jnp.exp(-gate))
    activated = gate * sigmoid_gate
    hidden = (activated * upper).astype(jnp.bfloat16)
    hid_ref[...] = hidden
    pay_ref[:, :model] = contract_cols(hidden, w_out).astype(jnp.bfloat16)
    grad_hidden = jnp.dot(recv_ref[:, model:], w_out, preferred_element_type=jnp.float32)
    grad_gate = grad_hidden * upper * sigmoid_gate * (1.0 + gate * (1.0 - sigmoid_gate))
    q_ref[:, :width] = grad_gate.astype(jnp.bfloat16)
    q_ref[:, width:] = (grad_hidden * activated).astype(jnp.bfloat16)
    pay_ref[:, model:] = contract_cols(q_ref[...], w_in).astype(jnp.bfloat16)


def expert_rows(recv, first, second):
    rows = recv.shape[0]
    model, width = second.shape
    chunks = 8 if model % 128 == 0 else 1
    vmem = pl.BlockSpec(memory_space=pltpu.VMEM)
    hbm = pl.BlockSpec(memory_space=pl.ANY)
    flops = 2 * rows * model * width * 6
    moved = 2 * (2 * rows * 2 * model + model * 3 * width + rows * 3 * width)
    return pl.pallas_call(
        expert_kernel,
        out_shape=(
            jax.ShapeDtypeStruct((rows, 2 * model), jnp.bfloat16),
            jax.ShapeDtypeStruct((rows, width), jnp.bfloat16),
            jax.ShapeDtypeStruct((rows, 2 * width), jnp.bfloat16),
        ),
        in_specs=[vmem, hbm, hbm],
        out_specs=(vmem, vmem, vmem),
        scratch_shapes=[
            pltpu.VMEM(first.shape, first.dtype),
            pltpu.VMEM(second.shape, second.dtype),
            pltpu.SemaphoreType.DMA((chunks + 1,)),
        ],
        compiler_params=pltpu.CompilerParams(vmem_limit_bytes=24 * 1024 * 1024),
        cost_estimate=pl.CostEstimate(
            flops=flops, bytes_accessed=moved, transcendentals=rows * width),
    )(
        pltpu.with_memory_space_constraint(recv, pltpu.VMEM),
        pltpu.with_memory_space_constraint(first, pltpu.HBM),
        pltpu.with_memory_space_constraint(second, pltpu.HBM),
    )


def dispatch_kernel(experts, route_hbm, weight_hbm, tokens_hbm, grad_hbm, send_ref,
                    gather_ref, column_ref, route_row_ref, weight_row_ref,
                    tokens_ref, grad_ref, sems):
    rows_in = [
        pltpu.make_async_copy(route_hbm, route_row_ref, sems.at[2]),
        pltpu.make_async_copy(weight_hbm, weight_row_ref, sems.at[3]),
    ]
    loads = [
        pltpu.make_async_copy(tokens_hbm, tokens_ref, sems.at[0]),
        pltpu.make_async_copy(grad_hbm, grad_ref, sems.at[1]),
    ]
    for load in rows_in + loads:
        load.start()
    for load in rows_in:
        load.wait()
    slot_count, count = send_ref.shape[0], route_row_ref.shape[1]
    capacity = slot_count // experts
    model = tokens_ref.shape[1]
    chosen = route_row_ref[...]
    kinds = lax.broadcasted_iota(jnp.int32, (experts, count), 0)
    onehot = (chosen == kinds).astype(jnp.bfloat16)
    earlier = (lax.broadcasted_iota(jnp.int32, (count, count), 0)
               < lax.broadcasted_iota(jnp.int32, (count, count), 1)).astype(jnp.bfloat16)
    before = jnp.dot(onehot, earlier, preferred_element_type=jnp.float32)
    ranks = jnp.sum(before * onehot.astype(jnp.float32), axis=0, keepdims=True).astype(jnp.int32)
    target = chosen * capacity + ranks
    slots = lax.broadcasted_iota(jnp.int32, (slot_count, count), 0)
    placer = (slots == target).astype(jnp.bfloat16)
    gather_ref[...] = jnp.transpose(placer)
    loads[0].wait()
    send_ref[:, :model] = jnp.dot(placer, tokens_ref[...], preferred_element_type=jnp.float32).astype(jnp.bfloat16)
    square = jnp.broadcast_to(weight_row_ref[...], (count, count))
    column = jnp.transpose(square)[:, :1]
    column_ref[...] = column
    loads[1].wait()
    cotangent = (column * grad_ref[...].astype(jnp.float32)).astype(jnp.bfloat16)
    send_ref[:, model:] = jnp.dot(placer, cotangent, preferred_element_type=jnp.float32).astype(jnp.bfloat16)


def dispatch_rows(routes, route_weight, tokens, out_grad, experts, capacity):
    count, model = tokens.shape
    vmem = pl.BlockSpec(memory_space=pltpu.VMEM)
    hbm = pl.BlockSpec(memory_space=pl.ANY)
    return pl.pallas_call(
        functools.partial(dispatch_kernel, experts),
        out_shape=(
            jax.ShapeDtypeStruct((experts * capacity, 2 * model), jnp.bfloat16),
            jax.ShapeDtypeStruct((count, experts * capacity), jnp.bfloat16),
            jax.ShapeDtypeStruct((count, 1), jnp.float32),
        ),
        in_specs=[hbm, hbm, hbm, hbm],
        out_specs=(vmem, vmem, vmem),
        scratch_shapes=[
            pltpu.VMEM((1, count), jnp.int32),
            pltpu.VMEM((1, count), jnp.float32),
            pltpu.VMEM(tokens.shape, tokens.dtype),
            pltpu.VMEM(out_grad.shape, out_grad.dtype),
            pltpu.SemaphoreType.DMA((4,)),
        ],
        compiler_params=pltpu.CompilerParams(vmem_limit_bytes=16 * 1024 * 1024),
        cost_estimate=pl.CostEstimate(
            flops=2 * experts * capacity * count * 2 * model,
            bytes_accessed=2 * (2 * count * model + experts * capacity * 2 * model),
            transcendentals=0),
    )(
        pltpu.with_memory_space_constraint(routes.reshape(1, count), pltpu.HBM),
        pltpu.with_memory_space_constraint(route_weight.reshape(1, count), pltpu.HBM),
        pltpu.with_memory_space_constraint(tokens, pltpu.HBM),
        pltpu.with_memory_space_constraint(out_grad, pltpu.HBM),
    )


def combine_kernel(back_ref, gather_ref, weight_ref, mixed_ref, grad_ref):
    model = mixed_ref.shape[1]
    gather = gather_ref[...]
    mixed_ref[...] = (weight_ref[...] * jnp.dot(
        gather, back_ref[:, :model], preferred_element_type=jnp.float32)).astype(jnp.bfloat16)
    grad_ref[...] = jnp.dot(
        gather, back_ref[:, model:], preferred_element_type=jnp.float32).astype(jnp.bfloat16)


def combine_rows(back, gather, route_weight):
    count, slot_count = gather.shape
    model = back.shape[1] // 2
    vmem = pl.BlockSpec(memory_space=pltpu.VMEM)
    return pl.pallas_call(
        combine_kernel,
        out_shape=(
            jax.ShapeDtypeStruct((count, model), jnp.bfloat16),
            jax.ShapeDtypeStruct((count, model), jnp.bfloat16),
        ),
        in_specs=[vmem] * 3,
        out_specs=(vmem, vmem),
        compiler_params=pltpu.CompilerParams(vmem_limit_bytes=16 * 1024 * 1024),
        cost_estimate=pl.CostEstimate(
            flops=2 * count * slot_count * 2 * model,
            bytes_accessed=2 * (slot_count * 2 * model + 2 * count * model),
            transcendentals=0),
    )(pltpu.with_memory_space_constraint(back, pltpu.VMEM), gather, route_weight)


def per_device(tokens, routes, route_weight, w_in, w_out, out_grad):
    token_count, model = tokens.shape
    experts = w_in.shape[0] * lax.axis_size("expert")
    capacity = 3 * token_count // (2 * experts)
    width = w_out.shape[2]
    replicas = lax.axis_size("dp")
    first = w_in[0]
    second = w_out[0]
    send, gather, column = dispatch_rows(routes, route_weight, tokens, out_grad, experts, capacity)
    recv = lax.all_to_all(send, "expert", split_axis=0, concat_axis=0, tiled=True)
    payload, hidden, grad_both = expert_rows(recv, first, second)
    rows_in = recv[:, :model]
    rows_cot = recv[:, model:]
    back = lax.all_to_all(payload, "expert", split_axis=0, concat_axis=0, tiled=True)
    mixed, token_grad = combine_rows(back, gather, column)
    halves = []
    for rows, right in ((rows_in, grad_both), (rows_cot, hidden)):
        ordered = halving_order(rows, "dp")
        middle = ordered.shape[1] // 2
        halves.append(tuple(
            contract_rows(piece, right).astype(jnp.bfloat16)
            for piece in (ordered[:, :middle], ordered[:, middle:])
        ))
    sum_first, sum_second = reduce_scatter_rows(halves, "dp")
    grad_in = (sum_first / replicas).astype(jnp.bfloat16)[None]
    grad_out = (sum_second / replicas).astype(jnp.bfloat16)[None]
    return (mixed, token_grad, grad_in, grad_out)


def solution(mesh):
    in_specs = (
        P(("expert", "dp"), None),
        P(("expert", "dp"), None),
        P(("expert", "dp"), None),
        P("expert", None, None),
        P("expert", None, None),
        P(("expert", "dp"), None),
    )
    out_specs = (
        P(("expert", "dp"), None),
        P(("expert", "dp"), None),
        P("expert", "dp", None),
        P("expert", "dp", None),
    )
    return jax.shard_map(
        per_device, mesh=mesh, in_specs=in_specs, out_specs=out_specs, check_vma=False
    )
```
